32 devices in a mesh: brick: 8 (over y, x, core), plane: 4 (over z).
Axes of the slice: x: 2, y: 2, z: 4, core: 2. Of those that a mesh axis runs over, the one named last changes fastest.
Arguments:
- positions: float32 [8, 4, 3, 4096], P('brick', 'plane'), may hold values from 0 to 64
- aux: float32 [8, 4, 4096], P('brick', 'plane'), may hold values from -1 to 1.8
- aux_prev: float32 [8, 4, 4096], P('brick', 'plane'), may hold values from -3 to 3
- resid: float32 [8, 4, 4096], P('brick', 'plane'), may hold values from -2 to 2
- types: int32 [8, 4, 4096], P('brick', 'plane'), may hold values from 0 to 7
- pair_tiles: int32 [8, 4, 1496], P('brick', 'plane'), may hold values from 0 to 63, as said below
- pair_cands: int32 [8, 4, 1496], P('brick', 'plane'), may hold values from 0 to 319, as said below
- pair_count: int32 [8, 4], P('brick', 'plane'), may hold values from 0 to 1496, as said below
- owner_tile: int32 [8, 4, 64], P('brick', 'plane'), may hold values from 0 to 255, as said below
- electroneg: float32 [8], replicated, may hold values from -3 to 3
- hardness: float32 [8], replicated, may hold values from 6 to 14
- widths: float32 [8], replicated, may hold values from 0.6 to 2
Outputs:
- charges: float32 [8, 4, 4096], P('brick', 'plane')
- next_aux: float32 [8, 4, 4096], P('brick', 'plane')
- resid_field: float32 [8, 4, 4096], P('brick', 'plane')
The draws below stay inside these ranges and needn't reach their ends.
Inputs may be any that keep to these rules, and one draw needn't show every extreme that they name: `pair_tiles`: entries after the first pair_count[b, p] of a brick's list are not used. `pair_cands`: A used pair never names a neighbour brick beyond the ends of the brick axis. `pair_count`: at most 1496 pairs a brick, reached by some brick. `owner_tile`: for each b the values over all p and t form a permutation of 0 to 255, and each brick (b, p) has exactly 16 tiles of each value // 64.
All inputs are finite; a program needn't handle non-finite values.
Results may differ from the reference program's by a relative error of at most 0.0003.
Values sent between devices are 32-bit elements; how exact they have to be, the bound alone decides.
No kernel may reach another device: no remote copies, remote signals or barrier semaphores. Data moves between devices by JAX's collectives and lax.ppermute only.
A program may use at most 64 MiB of HBM per device.

```python
import math
import jax
import jax.numpy as jnp
from jax import lax

TX = 2
TY = 4
TZ = 8
TILE = 64
NTYPES = 8
BRICKS = 8
PLANES = 4
ATOMS_DEV = 4096
PAIR_CAP = 1496


def pair_lists(key):
    base_key = jax.random.fold_in(key, 7)
    portion_key, ranking_key = jax.random.split(base_key)
    tile_count = TX * TY * TZ
    entries = tile_count * 27
    flat_index = jnp.arange(entries, dtype=jnp.int32)
    tile_of = flat_index // 27
    offset_of = flat_index % 27
    step_x = offset_of // 9 - 1
    step_y = offset_of // 3 % 3 - 1
    step_z = offset_of % 3 - 1
    home_x = tile_of // (TY * TZ)
    home_y = tile_of // TZ % TY
    home_z = tile_of % TZ
    reach_x = home_x + step_x
    reach_y = home_y + step_y
    reach_z = home_z + step_z
    below_x = reach_x < 0
    beyond_x = reach_x >= TX
    below_y = reach_y < 0
    beyond_y = reach_y >= TY
    cross_x = below_x | beyond_x
    cross_y = below_y | beyond_y
    inside = (reach_z >= 0) & (reach_z < TZ) & jnp.logical_not(cross_x & cross_y)
    block_of = jnp.where(below_x, 1, jnp.where(beyond_x, 2, jnp.where(below_y, 3, jnp.where(beyond_y, 4, 0))))
    partner = block_of * tile_count + (reach_x % TX * TY + reach_y % TY) * TZ + jnp.clip(reach_z, 0, TZ - 1)
    brick_of = jnp.arange(BRICKS, dtype=jnp.int32)[:, None, None]
    usable = inside[None, None, :] & jnp.logical_not(below_x[None, None, :] & (brick_of == 0))
    usable = usable & jnp.logical_not(beyond_x[None, None, :] & (brick_of == BRICKS - 1))
    usable = jnp.broadcast_to(usable, (BRICKS, PLANES, entries))
    crowded = brick_of >= 3 * BRICKS // 4
    portion = jnp.where(crowded, 20, jax.random.randint(portion_key, (BRICKS, PLANES, 1), 3, 7))
    usable_int = usable.astype(jnp.int32)
    pair_total = jnp.sum(usable_int, axis=-1, keepdims=True) * portion // 20
    scores = jax.random.randint(ranking_key, (BRICKS, PLANES, entries), 0, entries) * entries + flat_index[None, None, :]
    ranking = jnp.argsort(-(usable_int * entries * entries + scores), axis=-1)[:, :, :PAIR_CAP]
    chosen_tiles = jnp.take(tile_of, ranking)
    chosen_partners = jnp.take(partner, ranking)
    return (chosen_tiles.astype(jnp.int32), chosen_partners.astype(jnp.int32), pair_total[:, :, 0].astype(jnp.int32))


def draw_pair_tiles(key, part):
    return pair_lists(key)[0]


def draw_pair_cands(key, part):
    return pair_lists(key)[1]


def draw_pair_count(key, part):
    return pair_lists(key)[2]


def draw_owner_tile(key, part):
    tile_count = TX * TY * TZ
    quarter = tile_count // PLANES

    def one_brick(brick_key):
        source_key, slot_key = jax.random.split(brick_key)
        orders = jax.vmap(lambda inner: jax.random.permutation(inner, tile_count))(jax.random.split(source_key, PLANES))
        slots = jax.vmap(lambda inner: jax.random.permutation(inner, tile_count))(jax.random.split(slot_key, PLANES))
        position = jnp.arange(tile_count, dtype=jnp.int32)
        owner = position // quarter
        within = position % quarter
        source = jnp.arange(PLANES, dtype=jnp.int32)[:, None]
        value = owner[None, :] * tile_count + slots[owner[None, :], source * quarter + within[None, :]]
        return jnp.zeros((PLANES, tile_count), jnp.int32).at[source, orders].set(value.astype(jnp.int32))
    return jax.vmap(one_brick)(jax.random.split(jax.random.fold_in(key, 11), BRICKS))


def draw_positions(key, part):
    tile_count = TX * TY * TZ
    atom_index = jnp.arange(tile_count * TILE, dtype=jnp.int32)
    tile_of = atom_index // TILE
    cell_index = jnp.stack([tile_of // (TY * TZ), tile_of // TZ % TY, tile_of % TZ]).astype(jnp.float32)
    jitter = jax.random.uniform(jax.random.fold_in(key, 3), (BRICKS, PLANES, 3, tile_count * TILE), jnp.float32)
    return (cell_index[None, None] + jitter) * 8.0


def draw_aux(key, part):
    full_shape = (BRICKS, PLANES, TX * TY * TZ * TILE)
    level = jnp.arange(BRICKS, dtype=jnp.float32)[:, None, None] / (BRICKS - 1)
    inner = jax.random.fold_in(key, 5)
    jitter = 0.3 * jnp.clip(jax.random.normal(inner, full_shape, jnp.float32), -4.0, 4.0)
    center = 0.2 + 0.4 * level
    return center + jitter


def touch_ends(result, stream_key, least, largest):
    longest = result.shape.index(max(result.shape))
    spots = []
    for shift in (0, 1):
        where = [jax.random.randint(jax.random.fold_in(stream_key, axis), (), 0, length) for axis, length in enumerate(result.shape)]
        where[longest] = (where[longest] + shift) % result.shape[longest]
        spots.append(tuple(where))
    return result.at[spots[0]].set(least).at[spots[1]].set(largest)


def block_levels(rng, dims, cuts, smallest, largest):
    factor_of = 1.0
    for dim, shards_of in cuts:
        steps = jax.random.uniform(jax.random.fold_in(jax.random.fold_in(rng, 6), dim), (shards_of,), jnp.float32, smallest / len(cuts), largest / len(cuts))
        factor_of = factor_of * jnp.repeat(jnp.exp(steps), dims[dim] // shards_of).reshape((-1,) + (1,) * (len(dims) - 1 - dim))
    return factor_of


def centred(own_key, extent, deviation, bound, shards=(), kind=jnp.bfloat16):
    result = deviation * jax.random.normal(own_key, extent, jnp.float32)
    if shards:
        result = result * block_levels(own_key, extent, shards, -0.22, 0.18)
    return jnp.clip(result, -bound, bound).astype(kind)


def setup_inputs(seed: int = 0) -> dict:
    key_list = jax.random.split(jax.random.key(seed), 13)
    return {
        "positions": draw_positions(jax.random.fold_in(key_list[12], 71), 0),
        "aux": draw_aux(jax.random.fold_in(key_list[12], 71), 0),
        "aux_prev": centred(key_list[2], (BRICKS, PLANES, ATOMS_DEV), 0.5, 3.0, ((0, 8), (1, 4)), jnp.float32),
        "resid": centred(key_list[3], (BRICKS, PLANES, ATOMS_DEV), 0.3, 2.0, ((0, 8), (1, 4)), jnp.float32),
        "types": touch_ends(jax.random.randint(key_list[4], (BRICKS, PLANES, ATOMS_DEV), 0, NTYPES), jax.random.fold_in(key_list[4], 1), 0, NTYPES - 1).astype(jnp.int32),
        "pair_tiles": draw_pair_tiles(jax.random.fold_in(key_list[12], 71), 0),
        "pair_cands": draw_pair_cands(jax.random.fold_in(key_list[12], 71), 0),
        "pair_count": draw_pair_count(jax.random.fold_in(key_list[12], 71), 0),
        "owner_tile": draw_owner_tile(jax.random.fold_in(key_list[12], 71), 0),
        "electroneg": jnp.clip(jax.random.uniform(key_list[9], (NTYPES,), jnp.float32, -3.0, 3.0), -3.0, 3.0),
        "hardness": jnp.clip(jnp.exp(jax.random.uniform(key_list[10], (NTYPES,), jnp.float32, math.log(6.0), math.log(14.0))), 6.0, 14.0),
        "widths": jnp.clip(jnp.exp(jax.random.uniform(key_list[11], (NTYPES,), jnp.float32, math.log(0.6), math.log(2.0))), 0.6, 2.0),
    }


cell_edge = 8.0
cutoff = 10.0
soften = 0.5
kappa = 1.86
pair_group = 256

def lookup(type_table, type_row):
    chosen = (type_row[None, :] == jnp.arange(type_table.shape[0], dtype=jnp.int32)[:, None]).astype(type_table.dtype)
    return lax.optimization_barrier(jnp.sum(type_table[:, None] * chosen, axis=0))

def candidates(blocks, tile_count):
    joined = jnp.stack(blocks, axis=1)
    offsets = jnp.zeros((6, 5), jnp.float32)
    offsets = offsets.at[0, 1].set(-TX * cell_edge).at[0, 2].set(TX * cell_edge)
    offsets = offsets.at[1, 3].set(-TY * cell_edge).at[1, 4].set(TY * cell_edge)
    joined = joined + offsets[:, :, None]
    return joined.reshape(6, 5 * tile_count, TILE)

def pair_terms(home_tiles, candidate, near_ids, far_ids, in_range):
    tile_count = home_tiles.shape[1]
    near_atoms = jnp.take(home_tiles, near_ids, axis=1)
    far_atoms = jnp.take(candidate, far_ids, axis=1)
    delta_x = near_atoms[0][:, :, None] - far_atoms[0][:, None, :]
    delta_y = near_atoms[1][:, :, None] - far_atoms[1][:, None, :]
    delta_z = near_atoms[2][:, :, None] - far_atoms[2][:, None, :]
    dist_sq = delta_x * delta_x + delta_y * delta_y + delta_z * delta_z
    spacing = jnp.sqrt(dist_sq + soften * soften)
    inv_width = lax.rsqrt(near_atoms[5][:, :, None] ** 2 + far_atoms[5][:, None, :] ** 2)
    taper = jnp.square(jnp.maximum(1.0 - dist_sq / (cutoff * cutoff), 0.0))
    kernel = jax.scipy.special.erf(inv_width * spacing) / spacing * taper
    diagonal = jnp.arange(TILE, dtype=jnp.int32)[:, None] == jnp.arange(TILE, dtype=jnp.int32)[None, :]
    self_pairs = (far_ids == near_ids)[:, None, None] & diagonal[None]
    kept_pairs = in_range[:, None, None] & jnp.logical_not(self_pairs)
    kernel = jnp.where(kept_pairs, kernel, 0.0)
    pair_fields = jnp.einsum('pij,cpj->cpi', kernel, far_atoms[3:5], precision=lax.Precision.HIGHEST)
    chosen = (near_ids[:, None] == jnp.arange(tile_count, dtype=jnp.int32)[None, :]).astype(pair_fields.dtype)
    return jnp.einsum('pt,cpi->cti', chosen, pair_fields, precision=lax.Precision.HIGHEST)

def sweep_all(home_tiles, candidate, near_list, far_list, pair_total):
    extra = -PAIR_CAP % pair_group
    near_pad = jnp.concatenate([near_list, jnp.zeros((extra,), jnp.int32)]).reshape(-1, pair_group)
    far_pad = jnp.concatenate([far_list, jnp.zeros((extra,), jnp.int32)]).reshape(-1, pair_group)
    index_pad = jnp.arange(PAIR_CAP + extra, dtype=jnp.int32).reshape(-1, pair_group)

    def advance(running, block):
        near_ids, far_ids, indices = block
        return (running + pair_terms(home_tiles, candidate, near_ids, far_ids, indices < pair_total), None)
    start_total = jnp.zeros((2, home_tiles.shape[1], TILE), jnp.float32)
    running, unused = lax.scan(advance, start_total, (near_pad, far_pad, index_pad))
    return running

def reference(positions, aux, aux_prev, resid, types, pair_tiles, pair_cands, pair_count, owner_tile, electroneg, hardness, widths):
    tile_count = TX * TY * TZ
    atom_count = tile_count * TILE
    negativity = lookup(electroneg, types.reshape(-1)).reshape(types.shape)
    hardness_row = lookup(hardness, types.reshape(-1)).reshape(types.shape)
    radius = lookup(widths, types.reshape(-1)).reshape(types.shape)
    packed = jnp.concatenate([positions, aux[:, :, None], resid[:, :, None], radius[:, :, None]], axis=2)

    def one_device(index):
        brick_of = index // PLANES
        plane_of = index % PLANES
        below = (brick_of - 1) % BRICKS
        above = (brick_of + 1) % BRICKS
        left_side = (plane_of - 1) % PLANES
        right_side = (plane_of + 1) % PLANES
        blocks = [packed[brick_of, plane_of], packed[below, plane_of], packed[above, plane_of], packed[brick_of, left_side], packed[brick_of, right_side]]
        candidate = candidates(blocks, tile_count)
        home_tiles = blocks[0].reshape(6, tile_count, TILE)
        return sweep_all(home_tiles, candidate, pair_tiles[brick_of, plane_of], pair_cands[brick_of, plane_of], pair_count[brick_of, plane_of])
    fields = lax.map(one_device, jnp.arange(BRICKS * PLANES, dtype=jnp.int32))
    fields = fields.reshape(BRICKS, PLANES, 2, atom_count)
    aux_field = fields[:, :, 0]
    resid_field = fields[:, :, 1]
    field = negativity + aux_field + resid_field
    potential_level = (jnp.sum(aux) + jnp.sum(field / hardness_row)) / jnp.sum(1.0 / hardness_row)
    charges = (potential_level - field) / hardness_row
    group_tiles = PLANES * tile_count
    both = jnp.stack([aux, charges]).reshape(2, BRICKS, group_tiles, TILE)
    target = owner_tile.reshape(BRICKS, group_tiles)
    rows = jnp.arange(BRICKS, dtype=jnp.int32)[:, None]
    placed = jnp.zeros_like(both).at[:, rows, target].set(both)
    previous = aux_prev.reshape(BRICKS, group_tiles, TILE)
    next_aux = 2.0 * placed[0] - previous + kappa * (placed[1] - placed[0])
    return (charges, next_aux.reshape(BRICKS, PLANES, atom_count), resid_field)
```

```python
import jax
import jax.numpy as jnp
from jax import lax
from jax.sharding import PartitionSpec as P
from jax.experimental import pallas as pl
from jax.experimental.pallas import tpu as pltpu

TX = 2
TY = 4
TILE = 64


cell_edge = 8.0
cutoff = 10.0
soften = 0.5
kappa = 1.86
pair_group = 256


def shifted_from(block, axis, step):
    count = lax.axis_size(axis)
    pairs = [(i, (i + step) % count) for i in range(count)]
    return lax.ppermute(block, axis, pairs)


def neighbours(block):
    return [
        block,
        shifted_from(block, "brick", 1),
        shifted_from(block, "brick", -1),
        shifted_from(block, "plane", 1),
        shifted_from(block, "plane", -1),
    ]


def lookup(type_table, type_row):
    chosen = (
        type_row[None, :] == jnp.arange(type_table.shape[0], dtype=jnp.int32)[:, None]
    ).astype(type_table.dtype)
    return jnp.sum(type_table[:, None] * chosen, axis=0)


def candidates(blocks, tile_count):
    joined = jnp.stack(blocks, axis=1)
    offsets = jnp.zeros((6, 5), jnp.float32)
    offsets = offsets.at[0, 1].set(-TX * cell_edge).at[0, 2].set(TX * cell_edge)
    offsets = offsets.at[1, 3].set(-TY * cell_edge).at[1, 4].set(TY * cell_edge)
    joined = joined + offsets[:, :, None]
    return joined.reshape(6, 5 * tile_count, TILE)


LANES = 128


def sweep_kernel(near_ref, far_ref, count_ref, home_ref, cand_ref, out_ref, spread_ref, acc_ref):
    atom_count = home_ref.shape[0]
    tile_count = atom_count // TILE
    cand_tiles = cand_ref.shape[0]
    pair_cap = near_ref.shape[0]
    chunk = 512
    for q in range(4):
        for r in range(atom_count // chunk):
            column = home_ref[r * chunk:(r + 1) * chunk, q:q + 1]
            spread_ref[q, r * chunk:(r + 1) * chunk, :] = jnp.broadcast_to(column, (chunk, LANES))
    acc_ref[...] = jnp.zeros(acc_ref.shape, jnp.float32)
    total = count_ref[0]
    lane = lax.broadcasted_iota(jnp.int32, (1, LANES), 1)
    left = lane < TILE

    def body(k, carry):
        first = 2 * k
        second = jnp.minimum(first + 1, pair_cap - 1)
        has_second = first + 1 < total
        home_a = jnp.clip(near_ref[first], 0, tile_count - 1)
        cand_a = jnp.clip(far_ref[first], 0, cand_tiles - 1)
        home_b = jnp.clip(near_ref[second], 0, tile_count - 1)
        cand_b = jnp.clip(far_ref[second], 0, cand_tiles - 1)
        rows = jnp.where(left, cand_ref[cand_a], cand_ref[cand_b])
        base_a = pl.multiple_of(home_a * TILE, TILE)
        base_b = pl.multiple_of(home_b * TILE, TILE)

        def near_q(q):
            return jnp.where(
                left, spread_ref[q, pl.ds(base_a, TILE), :], spread_ref[q, pl.ds(base_b, TILE), :]
            )

        delta_x = near_q(0) - rows[0:1]
        delta_y = near_q(1) - rows[1:2]
        delta_z = near_q(2) - rows[2:3]
        dist_sq = delta_x * delta_x + delta_y * delta_y + delta_z * delta_z
        shifted = dist_sq + soften * soften
        inv_spacing = lax.rsqrt(shifted)
        spacing = shifted * inv_spacing
        inv_width = lax.rsqrt(near_q(3) + rows[3:4])
        taper = jnp.maximum(1.0 - dist_sq * (1.0 / (cutoff * cutoff)), 0.0)
        kernel = lax.erf(inv_width * spacing) * inv_spacing * (taper * taper)
        row_id = lax.broadcasted_iota(jnp.int32, (TILE, LANES), 0)
        lane_id = lax.broadcasted_iota(jnp.int32, (TILE, LANES), 1)
        self_a = (cand_a == home_a).astype(jnp.int32)
        self_b = (cand_b == home_b).astype(jnp.int32)
        self_half = jnp.where(lane_id < TILE, self_a, self_b)
        diagonal = (lane_id % TILE) == row_id
        kernel = jnp.where(diagonal & (self_half > 0), 0.0, kernel)
        keep_b = lane >= TILE + TILE * (1 - has_second.astype(jnp.int32))
        kernel_a = jnp.where(left, kernel, 0.0)
        kernel_b = jnp.where(keep_b, kernel, 0.0)
        for c in range(2):
            charge = rows[4 + c:5 + c]
            acc_ref[c, pl.ds(base_a, TILE), :] += kernel_a * charge
            acc_ref[c, pl.ds(base_b, TILE), :] += kernel_b * charge
        return carry

    lax.fori_loop(0, (total + 1) // 2, body, 0)
    ones = jnp.ones((8, LANES), jnp.float32)
    for c in range(2):
        summed = lax.dot_general(
            ones,
            acc_ref[c],
            (((1,), (1,)), ((), ())),
            precision=lax.Precision.HIGHEST,
            preferred_element_type=jnp.float32,
        )
        out_ref[c:c + 1, :] = summed[0:1]


def sweep(home_cols, cand_rows, near_list, far_list, pair_total):
    atom_count = home_cols.shape[0]
    smem = pl.BlockSpec(memory_space=pltpu.SMEM)
    vmem = pl.BlockSpec(memory_space=pltpu.VMEM)
    return pl.pallas_call(
        sweep_kernel,
        out_shape=jax.ShapeDtypeStruct((2, atom_count), jnp.float32),
        in_specs=[smem, smem, smem, vmem, vmem],
        out_specs=vmem,
        scratch_shapes=[
            pltpu.VMEM((4, atom_count, LANES), jnp.float32),
            pltpu.VMEM((2, atom_count, LANES), jnp.float32),
        ],
        compiler_params=pltpu.CompilerParams(vmem_limit_bytes=48 * 1024 * 1024),
    )(near_list, far_list, pair_total, home_cols, cand_rows)


def on_device(
    positions,
    aux,
    aux_prev,
    resid,
    types,
    pair_tiles,
    pair_cands,
    pair_count,
    owner_tile,
    electroneg,
    hardness,
    widths,
):
    atom_count = aux.shape[-1]
    tile_count = atom_count // TILE
    type_row = types.reshape(atom_count)
    negativity = lookup(electroneg, type_row)
    hardness_row = lookup(hardness, type_row)
    radius = lookup(widths, type_row)
    charge_row = aux.reshape(atom_count)
    resid_row = resid.reshape(atom_count)
    packed = jnp.concatenate(
        [positions.reshape(3, atom_count), charge_row[None], resid_row[None], radius[None]], axis=0
    )
    blocks = neighbours(packed)
    candidate = candidates(blocks, tile_count)
    cand_rows = jnp.concatenate(
        [candidate[:3], jnp.square(candidate[5:6]), candidate[3:5], jnp.zeros_like(candidate[:2])],
        axis=0,
    ).transpose(1, 0, 2)
    cand_rows = jnp.concatenate([cand_rows, cand_rows], axis=-1)
    home_cols = jnp.concatenate(
        [packed[:3], jnp.square(packed[5:6]), jnp.zeros_like(packed[:4])], axis=0
    ).T
    near_list = pair_tiles.reshape(-1)
    far_list = pair_cands.reshape(-1)
    pair_total = pair_count.reshape(1)
    totals = sweep(home_cols, cand_rows, near_list, far_list, pair_total)
    aux_field = totals[0].reshape(atom_count)
    resid_field = totals[1].reshape(atom_count)
    field = negativity + aux_field + resid_field
    global_sums = lax.psum(
        (jnp.sum(charge_row), jnp.sum(field / hardness_row), jnp.sum(1.0 / hardness_row)),
        ("brick", "plane"),
    )
    potential_level = (global_sums[0] + global_sums[1]) / global_sums[2]
    charges = (potential_level - field) / hardness_row
    stacked = jnp.stack([charge_row, charges]).reshape(2, tile_count, TILE)
    target = owner_tile.reshape(tile_count)
    planes = lax.axis_size("plane")
    quarter = tile_count // planes
    ranking = jnp.argsort(
        target // tile_count * tile_count + jnp.arange(tile_count, dtype=jnp.int32)
    )
    outgoing = jnp.take(stacked, ranking, axis=1).reshape(2, planes, quarter, TILE)
    slot_rows = (
        jnp.take(target % tile_count, ranking).astype(jnp.float32).reshape(1, planes, quarter)
    )
    arrived, arrived_slots = (
        lax.all_to_all(outgoing, "plane", split_axis=1, concat_axis=1, tiled=True),
        lax.all_to_all(slot_rows, "plane", split_axis=1, concat_axis=1, tiled=True),
    )
    arrived = arrived.reshape(2, tile_count, TILE)
    slot_ids = arrived_slots.reshape(tile_count).astype(jnp.int32)
    placer = (slot_ids[None, :] == jnp.arange(tile_count, dtype=jnp.int32)[:, None]).astype(
        jnp.float32
    )
    placed = jnp.einsum("sk,ckj->csj", placer, arrived, precision=lax.Precision.HIGHEST)
    previous = aux_prev.reshape(tile_count, TILE)
    next_aux = 2.0 * placed[0] - previous + kappa * (placed[1] - placed[0])
    return (charges.reshape(aux.shape), next_aux.reshape(aux.shape), resid_field.reshape(aux.shape))


def solution(mesh):
    in_specs = (
        P("brick", "plane", None, None),
        P("brick", "plane", None),
        P("brick", "plane", None),
        P("brick", "plane", None),
        P("brick", "plane", None),
        P("brick", "plane", None),
        P("brick", "plane", None),
        P("brick", "plane"),
        P("brick", "plane", None),
        P(),
        P(),
        P(),
    )
    out_specs = (P("brick", "plane", None), P("brick", "plane", None), P("brick", "plane", None))
    return jax.shard_map(
        on_device, mesh=mesh, in_specs=in_specs, out_specs=out_specs, check_vma=False
    )
```

```python
import jax
import jax.numpy as jnp
from jax import lax
from jax.sharding import PartitionSpec as P
from jax.experimental import pallas as pl
from jax.experimental.pallas import tpu as pltpu

TX = 2
TY = 4
TILE = 64


cell_edge = 8.0
cutoff = 10.0
soften = 0.5
kappa = 1.86
pair_group = 256


def shifted_from(block, axis, step):
    count = lax.axis_size(axis)
    pairs = [(i, (i + step) % count) for i in range(count)]
    return lax.ppermute(block, axis, pairs)


def neighbours(block):
    return [
        block,
        shifted_from(block, "brick", 1),
        shifted_from(block, "brick", -1),
        shifted_from(block, "plane", 1),
        shifted_from(block, "plane", -1),
    ]


def lookup(type_table, type_row):
    chosen = (
        type_row[None, :] == jnp.arange(type_table.shape[0], dtype=jnp.int32)[:, None]
    ).astype(type_table.dtype)
    return jnp.sum(type_table[:, None] * chosen, axis=0)


def candidates(blocks, tile_count):
    joined = jnp.stack(blocks, axis=1)
    offsets = jnp.zeros((6, 5), jnp.float32)
    offsets = offsets.at[0, 1].set(-TX * cell_edge).at[0, 2].set(TX * cell_edge)
    offsets = offsets.at[1, 3].set(-TY * cell_edge).at[1, 4].set(TY * cell_edge)
    joined = joined + offsets[:, :, None]
    return joined.reshape(6, 5 * tile_count, TILE)


LANES = 128


def sweep_kernel(near_ref, far_ref, count_ref, home_ref, cand_ref, out_ref, spread_ref, acc_ref):
    atom_count = home_ref.shape[0]
    tile_count = atom_count // TILE
    cand_tiles = cand_ref.shape[0]
    pair_cap = near_ref.shape[0]
    chunk = 512
    for q in range(4):
        for r in range(atom_count // chunk):
            column = home_ref[r * chunk:(r + 1) * chunk, q:q + 1]
            spread_ref[q, r * chunk:(r + 1) * chunk, :] = jnp.broadcast_to(column, (chunk, LANES))
    acc_ref[...] = jnp.zeros(acc_ref.shape, jnp.float32)
    total = count_ref[0]
    lane = lax.broadcasted_iota(jnp.int32, (1, LANES), 1)
    left = lane < TILE

    def body(k, carry):
        first = 2 * k
        second = jnp.minimum(first + 1, pair_cap - 1)
        has_second = first + 1 < total
        home_a = jnp.clip(near_ref[first], 0, tile_count - 1)
        cand_a = jnp.clip(far_ref[first], 0, cand_tiles - 1)
        home_b = jnp.clip(near_ref[second], 0, tile_count - 1)
        cand_b = jnp.clip(far_ref[second], 0, cand_tiles - 1)
        rows = jnp.where(left, cand_ref[cand_a], cand_ref[cand_b])
        base_a = pl.multiple_of(home_a * TILE, TILE)
        base_b = pl.multiple_of(home_b * TILE, TILE)

        def near_q(q):
            return jnp.where(
                left, spread_ref[q, pl.ds(base_a, TILE), :], spread_ref[q, pl.ds(base_b, TILE), :]
            )

        delta_x = near_q(0) - rows[0:1]
        delta_y = near_q(1) - rows[1:2]
        delta_z = near_q(2) - rows[2:3]
        dist_sq = delta_x * delta_x + delta_y * delta_y + delta_z * delta_z
        shifted = dist_sq + soften * soften
        inv_spacing = lax.rsqrt(shifted)
        spacing = shifted * inv_spacing
        inv_width = lax.rsqrt(near_q(3) + rows[3:4])
        taper = jnp.maximum(1.0 - dist_sq * (1.0 / (cutoff * cutoff)), 0.0)
        kernel = lax.erf(inv_width * spacing) * inv_spacing * (taper * taper)
        row_id = lax.broadcasted_iota(jnp.int32, (TILE, LANES), 0)
        lane_id = lax.broadcasted_iota(jnp.int32, (TILE, LANES), 1)
        self_a = (cand_a == home_a).astype(jnp.int32)
        self_b = (cand_b == home_b).astype(jnp.int32)
        self_half = jnp.where(lane_id < TILE, self_a, self_b)
        diagonal = (lane_id % TILE) == row_id
        kernel = jnp.where(diagonal & (self_half > 0), 0.0, kernel)
        keep_b = lane >= TILE + TILE * (1 - has_second.astype(jnp.int32))
        kernel_a = jnp.where(left, kernel, 0.0)
        kernel_b = jnp.where(keep_b, kernel, 0.0)
        for c in range(2):
            charge = rows[4 + c:5 + c]
            acc_ref[c, pl.ds(base_a, TILE), :] += kernel_a * charge
            acc_ref[c, pl.ds(base_b, TILE), :] += kernel_b * charge
        return carry

    lax.fori_loop(0, (total + 1) // 2, body, 0)
    ones = jnp.ones((8, LANES), jnp.float32)
    for c in range(2):
        summed = lax.dot_general(
            ones,
            acc_ref[c],
            (((1,), (1,)), ((), ())),
            precision=lax.Precision.HIGHEST,
            preferred_element_type=jnp.float32,
        )
        out_ref[c:c + 1, :] = summed[0:1]


def sweep(home_cols, cand_rows, near_list, far_list, pair_total):
    atom_count = home_cols.shape[0]
    smem = pl.BlockSpec(memory_space=pltpu.SMEM)
    vmem = pl.BlockSpec(memory_space=pltpu.VMEM)
    return pl.pallas_call(
        sweep_kernel,
        out_shape=jax.ShapeDtypeStruct((2, atom_count), jnp.float32),
        in_specs=[smem, smem, smem, vmem, vmem],
        out_specs=vmem,
        scratch_shapes=[
            pltpu.VMEM((4, atom_count, LANES), jnp.float32),
            pltpu.VMEM((2, atom_count, LANES), jnp.float32),
        ],
        compiler_params=pltpu.CompilerParams(vmem_limit_bytes=48 * 1024 * 1024),
    )(near_list, far_list, pair_total, home_cols, cand_rows)


def on_device(
    positions,
    aux,
    aux_prev,
    resid,
    types,
    pair_tiles,
    pair_cands,
    pair_count,
    owner_tile,
    electroneg,
    hardness,
    widths,
):
    atom_count = aux.shape[-1]
    tile_count = atom_count // TILE
    type_row = types.reshape(atom_count)
    negativity = lookup(electroneg, type_row)
    hardness_row = lookup(hardness, type_row)
    radius = lookup(widths, type_row)
    charge_row = aux.reshape(atom_count)
    resid_row = resid.reshape(atom_count)
    packed = jnp.concatenate(
        [positions.reshape(3, atom_count), charge_row[None], resid_row[None], radius[None]], axis=0
    )
    blocks = neighbours(packed)
    candidate = candidates(blocks, tile_count)
    cand_rows = jnp.concatenate(
        [candidate[:3], jnp.square(candidate[5:6]), candidate[3:5], jnp.zeros_like(candidate[:2])],
        axis=0,
    ).transpose(1, 0, 2)
    cand_rows = jnp.concatenate([cand_rows, cand_rows], axis=-1)
    home_cols = jnp.concatenate(
        [packed[:3], jnp.square(packed[5:6]), jnp.zeros_like(packed[:4])], axis=0
    ).T
    near_list = pair_tiles.reshape(-1)
    far_list = pair_cands.reshape(-1)
    pair_total = pair_count.reshape(1)
    totals = sweep(home_cols, cand_rows, near_list, far_list, pair_total)
    aux_field = totals[0].reshape(atom_count)
    resid_field = totals[1].reshape(atom_count)
    field = negativity + aux_field + resid_field
    planes = lax.axis_size("plane")
    devices = lax.axis_size("brick") * planes
    target = owner_tile.reshape(tile_count)
    placer = (
        target[:, None] == jnp.arange(planes * tile_count, dtype=jnp.int32)[None, :]
    ).astype(jnp.float32)

    def to_owners(rows):
        tiles = rows.reshape(rows.shape[0], tile_count, TILE)
        spread = jnp.einsum("tv,ctj->cvj", placer, tiles, precision=lax.Precision.HIGHEST)
        spread = spread.reshape(rows.shape[0], planes, tile_count, TILE)
        arrived = lax.all_to_all(spread, "plane", split_axis=1, concat_axis=1, tiled=True)
        return jnp.sum(arrived, axis=1)

    early = to_owners(jnp.stack([charge_row, hardness_row]))
    local_sums = jnp.stack(
        [jnp.sum(charge_row), jnp.sum(field / hardness_row), jnp.sum(1.0 / hardness_row)]
    )
    sums_out = jnp.broadcast_to(jnp.pad(local_sums, (0, 5))[None, :], (devices, 8))
    sums_in = lax.all_to_all(sums_out, ("brick", "plane"), split_axis=0, concat_axis=0, tiled=True)
    late = to_owners(field[None])
    global_sums = jnp.sum(sums_in, axis=0)
    potential_level = (global_sums[0] + global_sums[1]) / global_sums[2]
    charges = (potential_level - field) / hardness_row
    placed_aux = early[0]
    placed_charges = (potential_level - late[0]) / early[1]
    previous = aux_prev.reshape(tile_count, TILE)
    next_aux = 2.0 * placed_aux - previous + kappa * (placed_charges - placed_aux)
    return (charges.reshape(aux.shape), next_aux.reshape(aux.shape), resid_field.reshape(aux.shape))


def solution(mesh):
    in_specs = (
        P("brick", "plane", None, None),
        P("brick", "plane", None),
        P("brick", "plane", None),
        P("brick", "plane", None),
        P("brick", "plane", None),
        P("brick", "plane", None),
        P("brick", "plane", None),
        P("brick", "plane"),
        P("brick", "plane", None),
        P(),
        P(),
        P(),
    )
    out_specs = (P("brick", "plane", None), P("brick", "plane", None), P("brick", "plane", None))
    return jax.shard_map(
        on_device, mesh=mesh, in_specs=in_specs, out_specs=out_specs, check_vma=False
    )
```

```python
import numpy as np
import jax
import jax.numpy as jnp
from jax import lax
from jax.sharding import PartitionSpec as P
from jax.experimental import pallas as pl
from jax.experimental.pallas import tpu as pltpu

TX = 2
TY = 4
TILE = 64


cell_edge = 8.0
cutoff = 10.0
soften = 0.5
kappa = 1.86
pair_group = 256


def shifted_from(block, axis, step):
    count = lax.axis_size(axis)
    pairs = [(i, (i + step) % count) for i in range(count)]
    return lax.ppermute(block, axis, pairs)


def neighbours(block):
    return [
        block,
        shifted_from(block, "brick", 1),
        shifted_from(block, "brick", -1),
        shifted_from(block, "plane", 1),
        shifted_from(block, "plane", -1),
    ]


def lookup(type_table, type_row):
    chosen = (
        type_row[None, :] == jnp.arange(type_table.shape[0], dtype=jnp.int32)[:, None]
    ).astype(type_table.dtype)
    return jnp.sum(type_table[:, None] * chosen, axis=0)


def candidates(blocks, tile_count):
    joined = jnp.stack(blocks, axis=1)
    offsets = np.zeros((6, 5, 1), np.float32)
    offsets[0, 1] = -TX * cell_edge
    offsets[0, 2] = TX * cell_edge
    offsets[1, 3] = -TY * cell_edge
    offsets[1, 4] = TY * cell_edge
    joined = joined + offsets
    return joined.reshape(6, 5 * tile_count, TILE)


LANES = 128


def sweep_kernel(near_ref, far_ref, count_ref, home_ref, cand_ref, out_ref, spread_ref, acc_ref):
    atom_count = home_ref.shape[0]
    tile_count = atom_count // TILE
    cand_tiles = cand_ref.shape[0]
    pair_cap = near_ref.shape[0]
    chunk = 512
    for q in range(4):
        for r in range(atom_count // chunk):
            column = home_ref[r * chunk:(r + 1) * chunk, q:q + 1]
            spread_ref[q, r * chunk:(r + 1) * chunk, :] = jnp.broadcast_to(column, (chunk, LANES))
    acc_ref[...] = jnp.zeros(acc_ref.shape, jnp.float32)
    total = count_ref[0]
    lane = lax.broadcasted_iota(jnp.int32, (1, LANES), 1)
    left = lane < TILE

    def body(k, carry):
        first = 2 * k
        second = jnp.minimum(first + 1, pair_cap - 1)
        has_second = first + 1 < total
        home_a = jnp.clip(near_ref[first], 0, tile_count - 1)
        cand_a = jnp.clip(far_ref[first], 0, cand_tiles - 1)
        home_b = jnp.clip(near_ref[second], 0, tile_count - 1)
        cand_b = jnp.clip(far_ref[second], 0, cand_tiles - 1)
        rows = jnp.where(left, cand_ref[cand_a], cand_ref[cand_b])
        base_a = pl.multiple_of(home_a * TILE, TILE)
        base_b = pl.multiple_of(home_b * TILE, TILE)

        def near_q(q):
            return jnp.where(
                left, spread_ref[q, pl.ds(base_a, TILE), :], spread_ref[q, pl.ds(base_b, TILE), :]
            )

        delta_x = near_q(0) - rows[0:1]
        delta_y = near_q(1) - rows[1:2]
        delta_z = near_q(2) - rows[2:3]
        dist_sq = delta_x * delta_x + delta_y * delta_y + delta_z * delta_z
        shifted = dist_sq + soften * soften
        inv_spacing = lax.rsqrt(shifted)
        spacing = shifted * inv_spacing
        inv_width = lax.rsqrt(near_q(3) + rows[3:4])
        taper = jnp.maximum(1.0 - dist_sq * (1.0 / (cutoff * cutoff)), 0.0)
        kernel = lax.erf(inv_width * spacing) * inv_spacing * (taper * taper)
        row_id = lax.broadcasted_iota(jnp.int32, (TILE, LANES), 0)
        lane_id = lax.broadcasted_iota(jnp.int32, (TILE, LANES), 1)
        self_a = (cand_a == home_a).astype(jnp.int32)
        self_b = (cand_b == home_b).astype(jnp.int32)
        self_half = jnp.where(lane_id < TILE, self_a, self_b)
        diagonal = (lane_id % TILE) == row_id
        kernel = jnp.where(diagonal & (self_half > 0), 0.0, kernel)
        keep_b = lane >= TILE + TILE * (1 - has_second.astype(jnp.int32))
        kernel_a = jnp.where(left, kernel, 0.0)
        kernel_b = jnp.where(keep_b, kernel, 0.0)
        for c in range(2):
            charge = rows[4 + c:5 + c]
            acc_ref[c, pl.ds(base_a, TILE), :] += kernel_a * charge
            acc_ref[c, pl.ds(base_b, TILE), :] += kernel_b * charge
        return carry

    lax.fori_loop(0, (total + 1) // 2, body, 0)
    ones = jnp.ones((8, LANES), jnp.float32)
    for c in range(2):
        summed = lax.dot_general(
            ones,
            acc_ref[c],
            (((1,), (1,)), ((), ())),
            precision=lax.Precision.HIGHEST,
            preferred_element_type=jnp.float32,
        )
        out_ref[c:c + 1, :] = summed[0:1]


def sweep(home_cols, cand_rows, near_list, far_list, pair_total):
    atom_count = home_cols.shape[0]
    smem = pl.BlockSpec(memory_space=pltpu.SMEM)
    vmem = pl.BlockSpec(memory_space=pltpu.VMEM)
    return pl.pallas_call(
        sweep_kernel,
        out_shape=jax.ShapeDtypeStruct((2, atom_count), jnp.float32),
        in_specs=[smem, smem, smem, vmem, vmem],
        out_specs=vmem,
        scratch_shapes=[
            pltpu.VMEM((4, atom_count, LANES), jnp.float32),
            pltpu.VMEM((2, atom_count, LANES), jnp.float32),
        ],
        compiler_params=pltpu.CompilerParams(vmem_limit_bytes=48 * 1024 * 1024),
    )(near_list, far_list, pair_total, home_cols, cand_rows)


def on_device(
    positions,
    aux,
    aux_prev,
    resid,
    types,
    pair_tiles,
    pair_cands,
    pair_count,
    owner_tile,
    electroneg,
    hardness,
    widths,
):
    atom_count = aux.shape[-1]
    tile_count = atom_count // TILE
    type_row = types.reshape(atom_count)
    negativity = lookup(electroneg, type_row)
    hardness_row = lookup(hardness, type_row)
    radius = lookup(widths, type_row)
    charge_row = aux.reshape(atom_count)
    resid_row = resid.reshape(atom_count)
    packed = jnp.concatenate(
        [positions.reshape(3, atom_count), charge_row[None], resid_row[None], radius[None]], axis=0
    )
    blocks = neighbours(packed)
    candidate = candidates(blocks, tile_count)
    cand_rows = jnp.concatenate(
        [candidate[:3], jnp.square(candidate[5:6]), candidate[3:5], jnp.zeros_like(candidate[:2])],
        axis=0,
    ).transpose(1, 0, 2)
    cand_rows = jnp.concatenate([cand_rows, cand_rows], axis=-1)
    home_cols = jnp.concatenate(
        [packed[:3], jnp.square(packed[5:6]), jnp.zeros_like(packed[:4])], axis=0
    ).T
    near_list = pair_tiles.reshape(-1)
    far_list = pair_cands.reshape(-1)
    pair_total = pair_count.reshape(1)
    totals = sweep(home_cols, cand_rows, near_list, far_list, pair_total)
    aux_field = totals[0].reshape(atom_count)
    resid_field = totals[1].reshape(atom_count)
    field = negativity + aux_field + resid_field
    planes = lax.axis_size("plane")
    devices = lax.axis_size("brick") * planes
    target = owner_tile.reshape(tile_count)
    placer = (
        target[:, None] == jnp.arange(planes * tile_count, dtype=jnp.int32)[None, :]
    ).astype(jnp.float32)

    def to_owners(rows):
        tiles = rows.reshape(rows.shape[0], tile_count, TILE)
        spread = jnp.einsum("tv,ctj->cvj", placer, tiles, precision=lax.Precision.HIGHEST)
        spread = spread.reshape(rows.shape[0], planes, tile_count, TILE)
        arrived = lax.all_to_all(spread, "plane", split_axis=1, concat_axis=1, tiled=True)
        return jnp.sum(arrived, axis=1)

    local_sums = jnp.stack(
        [jnp.sum(charge_row), jnp.sum(field / hardness_row), jnp.sum(1.0 / hardness_row)]
    )
    sums_out = jnp.broadcast_to(jnp.pad(local_sums, (0, 5))[None, :], (devices, 8))
    sums_in = lax.all_to_all(sums_out, ("brick", "plane"), split_axis=0, concat_axis=0, tiled=True)
    placed = to_owners(jnp.stack([charge_row, hardness_row, field]))
    global_sums = jnp.sum(sums_in, axis=0)
    potential_level = (global_sums[0] + global_sums[1]) / global_sums[2]
    charges = (potential_level - field) / hardness_row
    placed_aux = placed[0]
    placed_charges = (potential_level - placed[2]) / placed[1]
    previous = aux_prev.reshape(tile_count, TILE)
    next_aux = 2.0 * placed_aux - previous + kappa * (placed_charges - placed_aux)
    return (charges.reshape(aux.shape), next_aux.reshape(aux.shape), resid_field.reshape(aux.shape))


def solution(mesh):
    in_specs = (
        P("brick", "plane", None, None),
        P("brick", "plane", None),
        P("brick", "plane", None),
        P("brick", "plane", None),
        P("brick", "plane", None),
        P("brick", "plane", None),
        P("brick", "plane", None),
        P("brick", "plane"),
        P("brick", "plane", None),
        P(),
        P(),
        P(),
    )
    out_specs = (P("brick", "plane", None), P("brick", "plane", None), P("brick", "plane", None))
    return jax.shard_map(
        on_device, mesh=mesh, in_specs=in_specs, out_specs=out_specs, check_vma=False
    )
```

```python
import numpy as np
import jax
import jax.numpy as jnp
from jax import lax
from jax.sharding import PartitionSpec as P
from jax.experimental import pallas as pl
from jax.experimental.pallas import tpu as pltpu

TX = 2
TY = 4
TILE = 64


cell_edge = 8.0
cutoff = 10.0
soften = 0.5
kappa = 1.86
pair_group = 256


def shifted_from(block, axis, step):
    count = lax.axis_size(axis)
    pairs = [(i, (i + step) % count) for i in range(count)]
    return lax.ppermute(block, axis, pairs)


def neighbours(block):
    return [
        block,
        shifted_from(block, "brick", 1),
        shifted_from(block, "brick", -1),
        shifted_from(block, "plane", 1),
        shifted_from(block, "plane", -1),
    ]


def lookup(type_table, type_row):
    chosen = (
        type_row[None, :] == jnp.arange(type_table.shape[0], dtype=jnp.int32)[:, None]
    ).astype(type_table.dtype)
    return jnp.sum(type_table[:, None] * chosen, axis=0)


def candidates(blocks, tile_count):
    joined = jnp.stack(blocks, axis=1)
    offsets = np.zeros((6, 5, 1), np.float32)
    offsets[0, 1] = -TX * cell_edge
    offsets[0, 2] = TX * cell_edge
    offsets[1, 3] = -TY * cell_edge
    offsets[1, 4] = TY * cell_edge
    joined = joined + offsets
    return joined.reshape(6, 5 * tile_count, TILE)


LANES = 128


def sweep_kernel(near_ref, far_ref, count_ref, home_ref, cand_ref, out_ref, spread_ref, acc_ref):
    atom_count = home_ref.shape[0]
    tile_count = atom_count // TILE
    cand_tiles = cand_ref.shape[0]
    pair_cap = near_ref.shape[0]
    chunk = 512
    for q in range(4):
        for r in range(atom_count // chunk):
            column = home_ref[r * chunk:(r + 1) * chunk, q:q + 1]
            spread_ref[q, r * chunk:(r + 1) * chunk, :] = jnp.broadcast_to(column, (chunk, LANES))
    acc_ref[...] = jnp.zeros(acc_ref.shape, jnp.float32)
    total = count_ref[0]
    lane = lax.broadcasted_iota(jnp.int32, (1, LANES), 1)
    left = lane < TILE
    lane_full = lax.broadcasted_iota(jnp.int32, (TILE, LANES), 1)
    left_full = lane_full < TILE
    right_full = jnp.logical_not(left_full)
    diagonal = (lane_full % TILE) == lax.broadcasted_iota(jnp.int32, (TILE, LANES), 0)

    def pair_kernel(first):
        second = jnp.minimum(first + 1, pair_cap - 1)
        has_first = (first < total).astype(jnp.float32)
        has_second = (first + 1 < total).astype(jnp.float32)
        first = jnp.minimum(first, pair_cap - 1)
        home_a = jnp.clip(near_ref[first], 0, tile_count - 1)
        cand_a = jnp.clip(far_ref[first], 0, cand_tiles - 1)
        home_b = jnp.clip(near_ref[second], 0, tile_count - 1)
        cand_b = jnp.clip(far_ref[second], 0, cand_tiles - 1)
        rows = jnp.where(left, cand_ref[cand_a] * has_first, cand_ref[cand_b] * has_second)
        base_a = pl.multiple_of(home_a * TILE, TILE)
        base_b = pl.multiple_of(home_b * TILE, TILE)

        def near_q(q):
            return jnp.where(
                left, spread_ref[q, pl.ds(base_a, TILE), :], spread_ref[q, pl.ds(base_b, TILE), :]
            )

        delta_x = near_q(0) - rows[0:1]
        delta_y = near_q(1) - rows[1:2]
        delta_z = near_q(2) - rows[2:3]
        dist_sq = delta_x * delta_x + delta_y * delta_y + delta_z * delta_z
        shifted = dist_sq + soften * soften
        inv_spacing = lax.rsqrt(shifted)
        spacing = shifted * inv_spacing
        inv_width = lax.rsqrt(near_q(3) + rows[3:4])
        taper = jnp.maximum(1.0 - dist_sq * (1.0 / (cutoff * cutoff)), 0.0)
        kernel = lax.erf(inv_width * spacing) * inv_spacing * (taper * taper)
        self_half = jnp.where(
            left, (cand_a == home_a).astype(jnp.int32), (cand_b == home_b).astype(jnp.int32)
        )
        kernel = jnp.where(diagonal & (self_half > 0), 0.0, kernel)
        return kernel, rows, base_a, base_b

    def accumulate(kernel, rows, base_a, base_b):
        for c in range(2):
            contribution = kernel * rows[4 + c:5 + c]
            slot_a = acc_ref.at[c, pl.ds(base_a, TILE), :]
            pltpu.store(slot_a, slot_a[...] + contribution, mask=left_full)
            slot_b = acc_ref.at[c, pl.ds(base_b, TILE), :]
            pltpu.store(slot_b, slot_b[...] + contribution, mask=right_full)

    def body(k, carry):
        parts = [pair_kernel(8 * k + 2 * u) for u in range(4)]
        for part in parts:
            accumulate(*part)
        return carry

    lax.fori_loop(0, (total + 7) // 8, body, 0)
    ones = jnp.ones((8, LANES), jnp.float32)
    for c in range(2):
        summed = lax.dot_general(
            ones,
            acc_ref[c],
            (((1,), (1,)), ((), ())),
            precision=lax.Precision.HIGHEST,
            preferred_element_type=jnp.float32,
        )
        out_ref[c:c + 1, :] = summed[0:1]


def sweep(home_cols, cand_rows, near_list, far_list, pair_total):
    atom_count = home_cols.shape[0]
    smem = pl.BlockSpec(memory_space=pltpu.SMEM)
    vmem = pl.BlockSpec(memory_space=pltpu.VMEM)
    return pl.pallas_call(
        sweep_kernel,
        out_shape=jax.ShapeDtypeStruct((2, atom_count), jnp.float32),
        in_specs=[smem, smem, smem, vmem, vmem],
        out_specs=vmem,
        scratch_shapes=[
            pltpu.VMEM((4, atom_count, LANES), jnp.float32),
            pltpu.VMEM((2, atom_count, LANES), jnp.float32),
        ],
        compiler_params=pltpu.CompilerParams(vmem_limit_bytes=48 * 1024 * 1024),
    )(near_list, far_list, pair_total, home_cols, cand_rows)


def on_device(
    positions,
    aux,
    aux_prev,
    resid,
    types,
    pair_tiles,
    pair_cands,
    pair_count,
    owner_tile,
    electroneg,
    hardness,
    widths,
):
    atom_count = aux.shape[-1]
    tile_count = atom_count // TILE
    type_row = types.reshape(atom_count)
    negativity = lookup(electroneg, type_row)
    hardness_row = lookup(hardness, type_row)
    radius = lookup(widths, type_row)
    charge_row = aux.reshape(atom_count)
    resid_row = resid.reshape(atom_count)
    packed = jnp.concatenate(
        [positions.reshape(3, atom_count), charge_row[None], resid_row[None], radius[None]], axis=0
    )
    blocks = neighbours(packed)
    candidate = candidates(blocks, tile_count)
    cand_rows = jnp.concatenate(
        [candidate[:3], jnp.square(candidate[5:6]), candidate[3:5], jnp.zeros_like(candidate[:2])],
        axis=0,
    ).transpose(1, 0, 2)
    cand_rows = jnp.concatenate([cand_rows, cand_rows], axis=-1)
    home_cols = jnp.concatenate(
        [packed[:3], jnp.square(packed[5:6]), jnp.zeros_like(packed[:4])], axis=0
    ).T
    near_list = pair_tiles.reshape(-1)
    far_list = pair_cands.reshape(-1)
    pair_total = pair_count.reshape(1)
    totals = sweep(home_cols, cand_rows, near_list, far_list, pair_total)
    aux_field = totals[0].reshape(atom_count)
    resid_field = totals[1].reshape(atom_count)
    field = negativity + aux_field + resid_field
    planes = lax.axis_size("plane")
    devices = lax.axis_size("brick") * planes
    target = owner_tile.reshape(tile_count)
    placer = (
        target[:, None] == jnp.arange(planes * tile_count, dtype=jnp.int32)[None, :]
    ).astype(jnp.float32)

    def to_owners(rows):
        tiles = rows.reshape(rows.shape[0], tile_count, TILE)
        spread = jnp.einsum("tv,ctj->cvj", placer, tiles, precision=lax.Precision.HIGHEST)
        spread = spread.reshape(rows.shape[0], planes, tile_count, TILE)
        arrived = lax.all_to_all(spread, "plane", split_axis=1, concat_axis=1, tiled=True)
        return jnp.sum(arrived, axis=1)

    local_sums = jnp.stack(
        [jnp.sum(charge_row), jnp.sum(field / hardness_row), jnp.sum(1.0 / hardness_row)]
    )
    sums_out = jnp.broadcast_to(jnp.pad(local_sums, (0, 5))[None, :], (devices, 8))
    sums_in = lax.all_to_all(sums_out, ("brick", "plane"), split_axis=0, concat_axis=0, tiled=True)
    placed = to_owners(jnp.stack([charge_row, hardness_row, field]))
    global_sums = jnp.sum(sums_in, axis=0)
    potential_level = (global_sums[0] + global_sums[1]) / global_sums[2]
    charges = (potential_level - field) / hardness_row
    placed_aux = placed[0]
    placed_charges = (potential_level - placed[2]) / placed[1]
    previous = aux_prev.reshape(tile_count, TILE)
    next_aux = 2.0 * placed_aux - previous + kappa * (placed_charges - placed_aux)
    return (charges.reshape(aux.shape), next_aux.reshape(aux.shape), resid_field.reshape(aux.shape))


def solution(mesh):
    in_specs = (
        P("brick", "plane", None, None),
        P("brick", "plane", None),
        P("brick", "plane", None),
        P("brick", "plane", None),
        P("brick", "plane", None),
        P("brick", "plane", None),
        P("brick", "plane", None),
        P("brick", "plane"),
        P("brick", "plane", None),
        P(),
        P(),
        P(),
    )
    out_specs = (P("brick", "plane", None), P("brick", "plane", None), P("brick", "plane", None))
    return jax.shard_map(
        on_device, mesh=mesh, in_specs=in_specs, out_specs=out_specs, check_vma=False
    )
```

```python
import numpy as np
import jax
import jax.numpy as jnp
from jax import lax
from jax.sharding import PartitionSpec as P
from jax.experimental import pallas as pl
from jax.experimental.pallas import tpu as pltpu

TX = 2
TY = 4
TILE = 64


cell_edge = 8.0
cutoff = 10.0
soften = 0.5
kappa = 1.86
pair_group = 256


def shifted_from(block, axis, step):
    count = lax.axis_size(axis)
    pairs = [(i, (i + step) % count) for i in range(count)]
    return lax.ppermute(block, axis, pairs)


def neighbours(block):
    return [
        block,
        shifted_from(block, "brick", 1),
        shifted_from(block, "brick", -1),
        shifted_from(block, "plane", 1),
        shifted_from(block, "plane", -1),
    ]


def lookup(type_table, type_row):
    chosen = (
        type_row[None, :] == jnp.arange(type_table.shape[0], dtype=jnp.int32)[:, None]
    ).astype(type_table.dtype)
    return jnp.sum(type_table[:, None] * chosen, axis=0)


def candidates(blocks, tile_count):
    joined = jnp.stack(blocks, axis=1)
    offsets = np.zeros((6, 5, 1), np.float32)
    offsets[0, 1] = -TX * cell_edge
    offsets[0, 2] = TX * cell_edge
    offsets[1, 3] = -TY * cell_edge
    offsets[1, 4] = TY * cell_edge
    joined = joined + offsets
    return joined.reshape(6, 5 * tile_count, TILE)


LANES = 128


def sweep_kernel(near_ref, far_ref, count_ref, home_ref, cand_ref, out_ref, spread_ref, acc_ref):
    atom_count = home_ref.shape[0]
    tile_count = atom_count // TILE
    cand_tiles = cand_ref.shape[0]
    pair_cap = near_ref.shape[0]
    chunk = 512
    for q in range(4):
        for r in range(atom_count // chunk):
            column = home_ref[r * chunk:(r + 1) * chunk, q:q + 1]
            spread_ref[q, r * chunk:(r + 1) * chunk, :] = jnp.broadcast_to(column, (chunk, LANES))
    acc_ref[...] = jnp.zeros(acc_ref.shape, jnp.float32)
    total = count_ref[0]
    lane = lax.broadcasted_iota(jnp.int32, (1, LANES), 1)
    left = lane < TILE
    lane_full = lax.broadcasted_iota(jnp.int32, (TILE, LANES), 1)
    left_full = lane_full < TILE
    right_full = jnp.logical_not(left_full)
    diagonal = (lane_full % TILE) == lax.broadcasted_iota(jnp.int32, (TILE, LANES), 0)

    def pair_kernel(first):
        second = jnp.minimum(first + 1, pair_cap - 1)
        has_first = (first < total).astype(jnp.float32)
        has_second = (first + 1 < total).astype(jnp.float32)
        first = jnp.minimum(first, pair_cap - 1)
        home_a = jnp.clip(near_ref[first], 0, tile_count - 1)
        cand_a = jnp.clip(far_ref[first], 0, cand_tiles - 1)
        home_b = jnp.clip(near_ref[second], 0, tile_count - 1)
        cand_b = jnp.clip(far_ref[second], 0, cand_tiles - 1)
        rows = jnp.where(left, cand_ref[cand_a] * has_first, cand_ref[cand_b] * has_second)
        base_a = pl.multiple_of(home_a * TILE, TILE)
        base_b = pl.multiple_of(home_b * TILE, TILE)

        def near_q(q):
            return jnp.where(
                left, spread_ref[q, pl.ds(base_a, TILE), :], spread_ref[q, pl.ds(base_b, TILE), :]
            )

        delta_x = near_q(0) - rows[0:1]
        delta_y = near_q(1) - rows[1:2]
        delta_z = near_q(2) - rows[2:3]
        dist_sq = delta_x * delta_x + delta_y * delta_y + delta_z * delta_z
        shifted = dist_sq + soften * soften
        inv_spacing = lax.rsqrt(shifted)
        spacing = shifted * inv_spacing
        inv_width = lax.rsqrt(near_q(3) + rows[3:4])
        taper = jnp.maximum(1.0 - dist_sq * (1.0 / (cutoff * cutoff)), 0.0)
        kernel = lax.erf(inv_width * spacing) * inv_spacing * (taper * taper)
        self_half = jnp.where(
            left, (cand_a == home_a).astype(jnp.int32), (cand_b == home_b).astype(jnp.int32)
        )
        kernel = jnp.where(diagonal & (self_half > 0), 0.0, kernel)
        return kernel, rows, base_a, base_b

    def accumulate(kernel, rows, base_a, base_b):
        for c in range(2):
            contribution = kernel * rows[4 + c:5 + c]
            slot_a = acc_ref.at[c, pl.ds(base_a, TILE), :]
            pltpu.store(slot_a, slot_a[...] + contribution, mask=left_full)
            slot_b = acc_ref.at[c, pl.ds(base_b, TILE), :]
            pltpu.store(slot_b, slot_b[...] + contribution, mask=right_full)

    def body(k, carry):
        parts = [pair_kernel(8 * k + 2 * u) for u in range(4)]
        for part in parts:
            accumulate(*part)
        return carry

    lax.fori_loop(0, (total + 7) // 8, body, 0)
    ones = jnp.ones((8, LANES), jnp.float32)
    for c in range(2):
        summed = lax.dot_general(
            ones,
            acc_ref[c],
            (((1,), (1,)), ((), ())),
            precision=lax.Precision.HIGHEST,
            preferred_element_type=jnp.float32,
        )
        out_ref[c:c + 1, :] = summed[0:1]


def sweep(home_cols, cand_rows, near_list, far_list, pair_total):
    atom_count = home_cols.shape[0]
    smem = pl.BlockSpec(memory_space=pltpu.SMEM)
    vmem = pl.BlockSpec(memory_space=pltpu.VMEM)
    return pl.pallas_call(
        sweep_kernel,
        out_shape=jax.ShapeDtypeStruct((2, atom_count), jnp.float32),
        in_specs=[smem, smem, smem, vmem, vmem],
        out_specs=vmem,
        scratch_shapes=[
            pltpu.VMEM((4, atom_count, LANES), jnp.float32),
            pltpu.VMEM((2, atom_count, LANES), jnp.float32),
        ],
        compiler_params=pltpu.CompilerParams(vmem_limit_bytes=48 * 1024 * 1024),
    )(near_list, far_list, pair_total, home_cols, cand_rows)


def on_device(
    positions,
    aux,
    aux_prev,
    resid,
    types,
    pair_tiles,
    pair_cands,
    pair_count,
    owner_tile,
    electroneg,
    hardness,
    widths,
):
    atom_count = aux.shape[-1]
    tile_count = atom_count // TILE
    type_row = types.reshape(atom_count)
    negativity = lookup(electroneg, type_row)
    hardness_row = lookup(hardness, type_row)
    radius = lookup(widths, type_row)
    charge_row = aux.reshape(atom_count)
    resid_row = resid.reshape(atom_count)
    packed = jnp.concatenate(
        [positions.reshape(3, atom_count), charge_row[None], resid_row[None], radius[None]], axis=0
    )
    blocks = neighbours(packed)
    candidate = candidates(blocks, tile_count)
    cand_rows = jnp.concatenate(
        [candidate[:3], jnp.square(candidate[5:6]), candidate[3:5], jnp.zeros_like(candidate[:2])],
        axis=0,
    ).transpose(1, 0, 2)
    cand_rows = jnp.concatenate([cand_rows, cand_rows], axis=-1)
    home_cols = jnp.concatenate(
        [packed[:3], jnp.square(packed[5:6]), jnp.zeros_like(packed[:4])], axis=0
    ).T
    near_list = pair_tiles.reshape(-1)
    far_list = pair_cands.reshape(-1)
    pair_total = pair_count.reshape(1)
    totals = sweep(home_cols, cand_rows, near_list, far_list, pair_total)
    aux_field = totals[0].reshape(atom_count)
    resid_field = totals[1].reshape(atom_count)
    field = negativity + aux_field + resid_field
    planes = lax.axis_size("plane")
    devices = lax.axis_size("brick") * planes
    target = owner_tile.reshape(tile_count)
    plane_index = lax.axis_index("plane")

    def to_owners(rows):
        tiles = rows.reshape(rows.shape[0], tile_count, TILE)
        total = None
        for step in range(planes):
            owner = (plane_index + step) % planes
            local_target = target - owner * tile_count
            placer = (
                local_target[:, None] == jnp.arange(tile_count, dtype=jnp.int32)[None, :]
            ).astype(jnp.float32)
            part = jnp.einsum("ts,ctj->csj", placer, tiles, precision=lax.Precision.HIGHEST)
            if step:
                part = lax.ppermute(
                    part, "plane", [(i, (i + step) % planes) for i in range(planes)]
                )
            total = part if total is None else total + part
        return total

    local_sums = jnp.stack(
        [jnp.sum(charge_row), jnp.sum(field / hardness_row), jnp.sum(1.0 / hardness_row)]
    )
    sums_out = jnp.broadcast_to(jnp.pad(local_sums, (0, 5))[None, :], (devices, 8))
    sums_in = lax.all_to_all(sums_out, ("brick", "plane"), split_axis=0, concat_axis=0, tiled=True)
    placed = to_owners(jnp.stack([charge_row, hardness_row, field]))
    global_sums = jnp.sum(sums_in, axis=0)
    potential_level = (global_sums[0] + global_sums[1]) / global_sums[2]
    charges = (potential_level - field) / hardness_row
    placed_aux = placed[0]
    placed_charges = (potential_level - placed[2]) / placed[1]
    previous = aux_prev.reshape(tile_count, TILE)
    next_aux = 2.0 * placed_aux - previous + kappa * (placed_charges - placed_aux)
    return (charges.reshape(aux.shape), next_aux.reshape(aux.shape), resid_field.reshape(aux.shape))


def solution(mesh):
    in_specs = (
        P("brick", "plane", None, None),
        P("brick", "plane", None),
        P("brick", "plane", None),
        P("brick", "plane", None),
        P("brick", "plane", None),
        P("brick", "plane", None),
        P("brick", "plane", None),
        P("brick", "plane"),
        P("brick", "plane", None),
        P(),
        P(),
        P(),
    )
    out_specs = (P("brick", "plane", None), P("brick", "plane", None), P("brick", "plane", None))
    return jax.shard_map(
        on_device, mesh=mesh, in_specs=in_specs, out_specs=out_specs, check_vma=False
    )
```

```python
import numpy as np
import jax
import jax.numpy as jnp
from jax import lax
from jax.sharding import PartitionSpec as P
from jax.experimental import pallas as pl
from jax.experimental.pallas import tpu as pltpu

TX = 2
TY = 4
TILE = 64


cell_edge = 8.0
cutoff = 10.0
soften = 0.5
kappa = 1.86
pair_group = 256


def shifted_from(block, axis, step):
    count = lax.axis_size(axis)
    pairs = [(i, (i + step) % count) for i in range(count)]
    return lax.ppermute(block, axis, pairs)


def neighbours(block):
    return [
        block,
        shifted_from(block, "brick", 1),
        shifted_from(block, "brick", -1),
        shifted_from(block, "plane", 1),
        shifted_from(block, "plane", -1),
    ]


def lookup(type_table, type_row):
    chosen = (
        type_row[None, :] == jnp.arange(type_table.shape[0], dtype=jnp.int32)[:, None]
    ).astype(type_table.dtype)
    return jnp.sum(type_table[:, None] * chosen, axis=0)


def candidates(blocks, tile_count):
    joined = jnp.stack(blocks, axis=1)
    offsets = np.zeros((6, 5, 1), np.float32)
    offsets[0, 1] = -TX * cell_edge
    offsets[0, 2] = TX * cell_edge
    offsets[1, 3] = -TY * cell_edge
    offsets[1, 4] = TY * cell_edge
    joined = joined + offsets
    return joined.reshape(6, 5 * tile_count, TILE)


LANES = 128


def sweep_kernel(near_ref, far_ref, count_ref, *refs):
    block_refs = refs[:5]
    out_ref, cand_ref, spread_ref, acc_ref = refs[5:]
    rows_per_block = block_refs[0].shape[0]
    atom_count = rows_per_block * LANES
    tile_count = atom_count // TILE
    cand_tiles = 5 * tile_count
    pair_cap = near_ref.shape[0]
    sublane = lax.broadcasted_iota(jnp.int32, (8, LANES), 0)
    shifts = ((0.0, 0.0), (-TX * cell_edge, 0.0), (TX * cell_edge, 0.0),
              (0.0, -TY * cell_edge), (0.0, TY * cell_edge))
    for k, (shift_x, shift_y) in enumerate(shifts):
        values = block_refs[k][...]
        if shift_x or shift_y:
            offset = jnp.where(sublane == 0, shift_x, jnp.where(sublane == 1, shift_y, 0.0))
            values = values + offset[None]
        cand_ref[k * rows_per_block:(k + 1) * rows_per_block] = values

    def spread_row(r, carry):
        columns = jnp.transpose(block_refs[0][r])
        start = pl.multiple_of(r * LANES, LANES)
        for q in range(4):
            spread_ref[q, pl.ds(start, LANES), :] = jnp.broadcast_to(
                columns[:, q:q + 1], (LANES, LANES)
            )
        return carry

    lax.fori_loop(0, rows_per_block, spread_row, 0)
    acc_ref[...] = jnp.zeros(acc_ref.shape, jnp.float32)
    total = count_ref[0]
    lane = lax.broadcasted_iota(jnp.int32, (1, LANES), 1)
    left = lane < TILE
    lane_full = lax.broadcasted_iota(jnp.int32, (TILE, LANES), 1)
    left_full = lane_full < TILE
    right_full = jnp.logical_not(left_full)
    diagonal = (lane_full % TILE) == lax.broadcasted_iota(jnp.int32, (TILE, LANES), 0)

    def pair_kernel(first):
        second = jnp.minimum(first + 1, pair_cap - 1)
        has_first = (first < total).astype(jnp.float32)
        has_second = (first + 1 < total).astype(jnp.float32)
        first = jnp.minimum(first, pair_cap - 1)
        home_a = jnp.clip(near_ref[first], 0, tile_count - 1)
        cand_a = jnp.clip(far_ref[first], 0, cand_tiles - 1)
        home_b = jnp.clip(near_ref[second], 0, tile_count - 1)
        cand_b = jnp.clip(far_ref[second], 0, cand_tiles - 1)
        row_a = cand_ref[cand_a // 2]
        row_a = jnp.where(cand_a % 2 == 1, pltpu.roll(row_a, TILE, 1), row_a)
        row_b = cand_ref[cand_b // 2]
        row_b = jnp.where(cand_b % 2 == 0, pltpu.roll(row_b, TILE, 1), row_b)
        rows = jnp.where(left, row_a * has_first, row_b * has_second)
        base_a = pl.multiple_of(home_a * TILE, TILE)
        base_b = pl.multiple_of(home_b * TILE, TILE)

        def near_q(q):
            return jnp.where(
                left, spread_ref[q, pl.ds(base_a, TILE), :], spread_ref[q, pl.ds(base_b, TILE), :]
            )

        delta_x = near_q(0) - rows[0:1]
        delta_y = near_q(1) - rows[1:2]
        delta_z = near_q(2) - rows[2:3]
        dist_sq = delta_x * delta_x + delta_y * delta_y + delta_z * delta_z
        shifted = dist_sq + soften * soften
        inv_spacing = lax.rsqrt(shifted)
        spacing = shifted * inv_spacing
        inv_width = lax.rsqrt(near_q(3) + rows[3:4])
        taper = jnp.maximum(1.0 - dist_sq * (1.0 / (cutoff * cutoff)), 0.0)
        kernel = lax.erf(inv_width * spacing) * inv_spacing * (taper * taper)
        self_half = jnp.where(
            left, (cand_a == home_a).astype(jnp.int32), (cand_b == home_b).astype(jnp.int32)
        )
        kernel = jnp.where(diagonal & (self_half > 0), 0.0, kernel)
        return kernel, rows, base_a, base_b

    def accumulate(kernel, rows, base_a, base_b):
        for c in range(2):
            contribution = kernel * rows[4 + c:5 + c]
            slot_a = acc_ref.at[c, pl.ds(base_a, TILE), :]
            pltpu.store(slot_a, slot_a[...] + contribution, mask=left_full)
            slot_b = acc_ref.at[c, pl.ds(base_b, TILE), :]
            pltpu.store(slot_b, slot_b[...] + contribution, mask=right_full)

    def body(k, carry):
        parts = [pair_kernel(8 * k + 2 * u) for u in range(4)]
        for part in parts:
            accumulate(*part)
        return carry

    lax.fori_loop(0, (total + 7) // 8, body, 0)
    ones = jnp.ones((8, LANES), jnp.float32)
    for c in range(2):
        summed = lax.dot_general(
            ones,
            acc_ref[c],
            (((1,), (1,)), ((), ())),
            precision=lax.Precision.HIGHEST,
            preferred_element_type=jnp.float32,
        )
        out_ref[c:c + 1, :] = summed[0:1]


def sweep(blocks, near_list, far_list, pair_total):
    rows_per_block = blocks[0].shape[0]
    atom_count = rows_per_block * LANES
    smem = pl.BlockSpec(memory_space=pltpu.SMEM)
    vmem = pl.BlockSpec(memory_space=pltpu.VMEM)
    return pl.pallas_call(
        sweep_kernel,
        out_shape=jax.ShapeDtypeStruct((2, atom_count), jnp.float32),
        in_specs=[smem, smem, smem] + [vmem] * 5,
        out_specs=vmem,
        scratch_shapes=[
            pltpu.VMEM((5 * rows_per_block, 8, LANES), jnp.float32),
            pltpu.VMEM((4, atom_count, LANES), jnp.float32),
            pltpu.VMEM((2, atom_count, LANES), jnp.float32),
        ],
        compiler_params=pltpu.CompilerParams(vmem_limit_bytes=48 * 1024 * 1024),
    )(near_list, far_list, pair_total, *blocks)


def on_device(
    positions,
    aux,
    aux_prev,
    resid,
    types,
    pair_tiles,
    pair_cands,
    pair_count,
    owner_tile,
    electroneg,
    hardness,
    widths,
):
    atom_count = aux.shape[-1]
    tile_count = atom_count // TILE
    type_row = types.reshape(atom_count)
    negativity = lookup(electroneg, type_row)
    hardness_row = lookup(hardness, type_row)
    radius = lookup(widths, type_row)
    charge_row = aux.reshape(atom_count)
    resid_row = resid.reshape(atom_count)
    packed = jnp.concatenate(
        [
            positions.reshape(3, atom_count),
            jnp.square(radius)[None],
            charge_row[None],
            resid_row[None],
            jnp.zeros((2, atom_count), jnp.float32),
        ],
        axis=0,
    )
    packed = packed.reshape(8, atom_count // LANES, LANES).transpose(1, 0, 2)
    blocks = neighbours(packed)
    near_list = pair_tiles.reshape(-1)
    far_list = pair_cands.reshape(-1)
    pair_total = pair_count.reshape(1)
    totals = sweep(blocks, near_list, far_list, pair_total)
    aux_field = totals[0].reshape(atom_count)
    resid_field = totals[1].reshape(atom_count)
    field = negativity + aux_field + resid_field
    planes = lax.axis_size("plane")
    devices = lax.axis_size("brick") * planes
    target = owner_tile.reshape(tile_count)
    plane_index = lax.axis_index("plane")

    def to_owners(rows):
        tiles = rows.reshape(rows.shape[0], tile_count, TILE)
        total = None
        for step in range(planes):
            owner = (plane_index + step) % planes
            local_target = target - owner * tile_count
            placer = (
                local_target[:, None] == jnp.arange(tile_count, dtype=jnp.int32)[None, :]
            ).astype(jnp.float32)
            part = jnp.einsum("ts,ctj->csj", placer, tiles, precision=lax.Precision.HIGHEST)
            if step:
                part = lax.ppermute(
                    part, "plane", [(i, (i + step) % planes) for i in range(planes)]
                )
            total = part if total is None else total + part
        return total

    local_sums = jnp.stack(
        [jnp.sum(charge_row), jnp.sum(field / hardness_row), jnp.sum(1.0 / hardness_row)]
    )
    sums_out = jnp.broadcast_to(jnp.pad(local_sums, (0, 5))[None, :], (devices, 8))
    sums_in = lax.all_to_all(sums_out, ("brick", "plane"), split_axis=0, concat_axis=0, tiled=True)
    placed = to_owners(jnp.stack([charge_row, hardness_row, field]))
    global_sums = jnp.sum(sums_in, axis=0)
    potential_level = (global_sums[0] + global_sums[1]) / global_sums[2]
    charges = (potential_level - field) / hardness_row
    placed_aux = placed[0]
    placed_charges = (potential_level - placed[2]) / placed[1]
    previous = aux_prev.reshape(tile_count, TILE)
    next_aux = 2.0 * placed_aux - previous + kappa * (placed_charges - placed_aux)
    return (charges.reshape(aux.shape), next_aux.reshape(aux.shape), resid_field.reshape(aux.shape))


def solution(mesh):
    in_specs = (
        P("brick", "plane", None, None),
        P("brick", "plane", None),
        P("brick", "plane", None),
        P("brick", "plane", None),
        P("brick", "plane", None),
        P("brick", "plane", None),
        P("brick", "plane", None),
        P("brick", "plane"),
        P("brick", "plane", None),
        P(),
        P(),
        P(),
    )
    out_specs = (P("brick", "plane", None), P("brick", "plane", None), P("brick", "plane", None))
    return jax.shard_map(
        on_device, mesh=mesh, in_specs=in_specs, out_specs=out_specs, check_vma=False
    )
```

```python
import numpy as np
import jax
import jax.numpy as jnp
from jax import lax
from jax.sharding import PartitionSpec as P
from jax.experimental import pallas as pl
from jax.experimental.pallas import tpu as pltpu

TX = 2
TY = 4
TILE = 64


cell_edge = 8.0
cutoff = 10.0
soften = 0.5
kappa = 1.86
pair_group = 256


def shifted_from(block, axis, step):
    count = lax.axis_size(axis)
    pairs = [(i, (i + step) % count) for i in range(count)]
    return lax.ppermute(block, axis, pairs)


def neighbours(block):
    return [
        block,
        shifted_from(block, "brick", 1),
        shifted_from(block, "brick", -1),
        shifted_from(block, "plane", 1),
        shifted_from(block, "plane", -1),
    ]


def lookup(type_table, type_row):
    chosen = (
        type_row[None, :] == jnp.arange(type_table.shape[0], dtype=jnp.int32)[:, None]
    ).astype(type_table.dtype)
    return jnp.sum(type_table[:, None] * chosen, axis=0)


def candidates(blocks, tile_count):
    joined = jnp.stack(blocks, axis=1)
    offsets = np.zeros((6, 5, 1), np.float32)
    offsets[0, 1] = -TX * cell_edge
    offsets[0, 2] = TX * cell_edge
    offsets[1, 3] = -TY * cell_edge
    offsets[1, 4] = TY * cell_edge
    joined = joined + offsets
    return joined.reshape(6, 5 * tile_count, TILE)


LANES = 128


def sweep_kernel(near_ref, far_ref, count_ref, home_ref, *refs):
    block_refs = refs[:5]
    out_ref, cand_ref, spread_ref, acc_ref = refs[5:]
    rows_per_block = block_refs[0].shape[0]
    atom_count = rows_per_block * LANES
    tile_count = atom_count // TILE
    cand_tiles = 5 * tile_count
    pair_cap = near_ref.shape[0]
    sublane = lax.broadcasted_iota(jnp.int32, (8, LANES), 0)
    left_rows = lax.broadcasted_iota(jnp.int32, (8, LANES), 1) < TILE
    shifts = ((0.0, 0.0), (-TX * cell_edge, 0.0), (TX * cell_edge, 0.0),
              (0.0, -TY * cell_edge), (0.0, TY * cell_edge))

    def build_rows(r, carry):
        for k, (shift_x, shift_y) in enumerate(shifts):
            values = block_refs[k][r]
            if shift_x or shift_y:
                values = values + jnp.where(
                    sublane == 0, shift_x, jnp.where(sublane == 1, shift_y, 0.0)
                )
            rolled = pltpu.roll(values, TILE, 1)
            cand_ref[k * tile_count + 2 * r] = jnp.where(left_rows, values, rolled)
            cand_ref[k * tile_count + 2 * r + 1] = jnp.where(left_rows, rolled, values)
        return carry

    lax.fori_loop(0, rows_per_block, build_rows, 0)
    chunk = 512
    for q in range(4):
        for r in range(atom_count // chunk):
            column = home_ref[r * chunk:(r + 1) * chunk, q:q + 1]
            spread_ref[q, r * chunk:(r + 1) * chunk, :] = jnp.broadcast_to(column, (chunk, LANES))
    acc_ref[...] = jnp.zeros(acc_ref.shape, jnp.float32)
    total = count_ref[0]
    lane = lax.broadcasted_iota(jnp.int32, (1, LANES), 1)
    left = lane < TILE
    lane_full = lax.broadcasted_iota(jnp.int32, (TILE, LANES), 1)
    left_full = lane_full < TILE
    right_full = jnp.logical_not(left_full)
    diagonal = (lane_full % TILE) == lax.broadcasted_iota(jnp.int32, (TILE, LANES), 0)

    def pair_kernel(first):
        second = jnp.minimum(first + 1, pair_cap - 1)
        has_first = (first < total).astype(jnp.float32)
        has_second = (first + 1 < total).astype(jnp.float32)
        first = jnp.minimum(first, pair_cap - 1)
        home_a = jnp.clip(near_ref[first], 0, tile_count - 1)
        cand_a = jnp.clip(far_ref[first], 0, cand_tiles - 1)
        home_b = jnp.clip(near_ref[second], 0, tile_count - 1)
        cand_b = jnp.clip(far_ref[second], 0, cand_tiles - 1)
        rows = jnp.where(left, cand_ref[cand_a] * has_first, cand_ref[cand_b] * has_second)
        base_a = pl.multiple_of(home_a * TILE, TILE)
        base_b = pl.multiple_of(home_b * TILE, TILE)

        def near_q(q):
            return jnp.where(
                left, spread_ref[q, pl.ds(base_a, TILE), :], spread_ref[q, pl.ds(base_b, TILE), :]
            )

        delta_x = near_q(0) - rows[0:1]
        delta_y = near_q(1) - rows[1:2]
        delta_z = near_q(2) - rows[2:3]
        dist_sq = delta_x * delta_x + delta_y * delta_y + delta_z * delta_z
        shifted = dist_sq + soften * soften
        inv_spacing = lax.rsqrt(shifted)
        spacing = shifted * inv_spacing
        inv_width = lax.rsqrt(near_q(3) + rows[3:4])
        taper = jnp.maximum(1.0 - dist_sq * (1.0 / (cutoff * cutoff)), 0.0)
        kernel = lax.erf(inv_width * spacing) * inv_spacing * (taper * taper)
        self_half = jnp.where(
            left, (cand_a == home_a).astype(jnp.int32), (cand_b == home_b).astype(jnp.int32)
        )
        kernel = jnp.where(diagonal & (self_half > 0), 0.0, kernel)
        return kernel, rows, base_a, base_b

    def accumulate(kernel, rows, base_a, base_b):
        for c in range(2):
            contribution = kernel * rows[4 + c:5 + c]
            slot_a = acc_ref.at[c, pl.ds(base_a, TILE), :]
            pltpu.store(slot_a, slot_a[...] + contribution, mask=left_full)
            slot_b = acc_ref.at[c, pl.ds(base_b, TILE), :]
            pltpu.store(slot_b, slot_b[...] + contribution, mask=right_full)

    def body(k, carry):
        parts = [pair_kernel(8 * k + 2 * u) for u in range(4)]
        for part in parts:
            accumulate(*part)
        return carry

    lax.fori_loop(0, (total + 7) // 8, body, 0)
    ones = jnp.ones((8, LANES), jnp.float32)
    for c in range(2):
        summed = lax.dot_general(
            ones,
            acc_ref[c],
            (((1,), (1,)), ((), ())),
            precision=lax.Precision.HIGHEST,
            preferred_element_type=jnp.float32,
        )
        out_ref[c:c + 1, :] = summed[0:1]


def sweep(home_cols, blocks, near_list, far_list, pair_total):
    rows_per_block = blocks[0].shape[0]
    atom_count = rows_per_block * LANES
    smem = pl.BlockSpec(memory_space=pltpu.SMEM)
    vmem = pl.BlockSpec(memory_space=pltpu.VMEM)
    return pl.pallas_call(
        sweep_kernel,
        out_shape=jax.ShapeDtypeStruct((2, atom_count), jnp.float32),
        in_specs=[smem, smem, smem] + [vmem] * 6,
        out_specs=vmem,
        scratch_shapes=[
            pltpu.VMEM((10 * rows_per_block, 8, LANES), jnp.float32),
            pltpu.VMEM((4, atom_count, LANES), jnp.float32),
            pltpu.VMEM((2, atom_count, LANES), jnp.float32),
        ],
        compiler_params=pltpu.CompilerParams(vmem_limit_bytes=48 * 1024 * 1024),
    )(near_list, far_list, pair_total, home_cols, *blocks)


def on_device(
    positions,
    aux,
    aux_prev,
    resid,
    types,
    pair_tiles,
    pair_cands,
    pair_count,
    owner_tile,
    electroneg,
    hardness,
    widths,
):
    atom_count = aux.shape[-1]
    tile_count = atom_count // TILE
    type_row = types.reshape(atom_count)
    negativity = lookup(electroneg, type_row)
    hardness_row = lookup(hardness, type_row)
    radius = lookup(widths, type_row)
    charge_row = aux.reshape(atom_count)
    resid_row = resid.reshape(atom_count)
    packed = jnp.concatenate(
        [
            positions.reshape(3, atom_count),
            jnp.square(radius)[None],
            charge_row[None],
            resid_row[None],
            jnp.zeros((2, atom_count), jnp.float32),
        ],
        axis=0,
    )
    home_cols = packed.T
    packed = packed.reshape(8, atom_count // LANES, LANES).transpose(1, 0, 2)
    blocks = neighbours(packed)
    near_list = pair_tiles.reshape(-1)
    far_list = pair_cands.reshape(-1)
    pair_total = pair_count.reshape(1)
    totals = sweep(home_cols, blocks, near_list, far_list, pair_total)
    aux_field = totals[0].reshape(atom_count)
    resid_field = totals[1].reshape(atom_count)
    field = negativity + aux_field + resid_field
    planes = lax.axis_size("plane")
    devices = lax.axis_size("brick") * planes
    target = owner_tile.reshape(tile_count)
    plane_index = lax.axis_index("plane")

    def to_owners(rows):
        tiles = rows.reshape(rows.shape[0], tile_count, TILE)
        total = None
        for step in range(planes):
            owner = (plane_index + step) % planes
            local_target = target - owner * tile_count
            placer = (
                local_target[:, None] == jnp.arange(tile_count, dtype=jnp.int32)[None, :]
            ).astype(jnp.float32)
            part = jnp.einsum("ts,ctj->csj", placer, tiles, precision=lax.Precision.HIGHEST)
            if step:
                part = lax.ppermute(
                    part, "plane", [(i, (i + step) % planes) for i in range(planes)]
                )
            total = part if total is None else total + part
        return total

    local_sums = jnp.stack(
        [jnp.sum(charge_row), jnp.sum(field / hardness_row), jnp.sum(1.0 / hardness_row)]
    )
    sums_out = jnp.broadcast_to(jnp.pad(local_sums, (0, 5))[None, :], (devices, 8))
    sums_in = lax.all_to_all(sums_out, ("brick", "plane"), split_axis=0, concat_axis=0, tiled=True)
    placed = to_owners(jnp.stack([charge_row, hardness_row, field]))
    global_sums = jnp.sum(sums_in, axis=0)
    potential_level = (global_sums[0] + global_sums[1]) / global_sums[2]
    charges = (potential_level - field) / hardness_row
    placed_aux = placed[0]
    placed_charges = (potential_level - placed[2]) / placed[1]
    previous = aux_prev.reshape(tile_count, TILE)
    next_aux = 2.0 * placed_aux - previous + kappa * (placed_charges - placed_aux)
    return (charges.reshape(aux.shape), next_aux.reshape(aux.shape), resid_field.reshape(aux.shape))


def solution(mesh):
    in_specs = (
        P("brick", "plane", None, None),
        P("brick", "plane", None),
        P("brick", "plane", None),
        P("brick", "plane", None),
        P("brick", "plane", None),
        P("brick", "plane", None),
        P("brick", "plane", None),
        P("brick", "plane"),
        P("brick", "plane", None),
        P(),
        P(),
        P(),
    )
    out_specs = (P("brick", "plane", None), P("brick", "plane", None), P("brick", "plane", None))
    return jax.shard_map(
        on_device, mesh=mesh, in_specs=in_specs, out_specs=out_specs, check_vma=False
    )
```

```python
import numpy as np
import jax
import jax.numpy as jnp
from jax import lax
from jax.sharding import PartitionSpec as P
from jax.experimental import pallas as pl
from jax.experimental.pallas import tpu as pltpu

TX = 2
TY = 4
TILE = 64


cell_edge = 8.0
cutoff = 10.0
soften = 0.5
kappa = 1.86
pair_group = 256


def shifted_from(block, axis, step):
    count = lax.axis_size(axis)
    pairs = [(i, (i + step) % count) for i in range(count)]
    return lax.ppermute(block, axis, pairs)


def neighbours(block):
    return [
        block,
        shifted_from(block, "brick", 1),
        shifted_from(block, "brick", -1),
        shifted_from(block, "plane", 1),
        shifted_from(block, "plane", -1),
    ]


def lookup(type_table, type_row):
    chosen = (
        type_row[None, :] == jnp.arange(type_table.shape[0], dtype=jnp.int32)[:, None]
    ).astype(type_table.dtype)
    return jnp.sum(type_table[:, None] * chosen, axis=0)


def candidates(blocks, tile_count):
    joined = jnp.stack(blocks, axis=1)
    offsets = np.zeros((6, 5, 1), np.float32)
    offsets[0, 1] = -TX * cell_edge
    offsets[0, 2] = TX * cell_edge
    offsets[1, 3] = -TY * cell_edge
    offsets[1, 4] = TY * cell_edge
    joined = joined + offsets
    return joined.reshape(6, 5 * tile_count, TILE)


LANES = 128


def sweep_kernel(near_ref, far_ref, count_ref, home_ref, *refs):
    block_refs = refs[:5]
    out_ref, cand_ref, spread_ref, acc_ref = refs[5:]
    rows_per_block = block_refs[0].shape[0]
    atom_count = rows_per_block * LANES
    tile_count = atom_count // TILE
    cand_tiles = 5 * tile_count
    pair_cap = near_ref.shape[-1]
    sublane = lax.broadcasted_iota(jnp.int32, (8, LANES), 0)
    left_rows = lax.broadcasted_iota(jnp.int32, (8, LANES), 1) < TILE
    shifts = ((0.0, 0.0), (-TX * cell_edge, 0.0), (TX * cell_edge, 0.0),
              (0.0, -TY * cell_edge), (0.0, TY * cell_edge))

    def build_rows(r, carry):
        for k, (shift_x, shift_y) in enumerate(shifts):
            values = block_refs[k][r]
            if shift_x or shift_y:
                values = values + jnp.where(
                    sublane == 0, shift_x, jnp.where(sublane == 1, shift_y, 0.0)
                )
            rolled = pltpu.roll(values, TILE, 1)
            cand_ref[k * tile_count + 2 * r] = jnp.where(left_rows, values, rolled)
            cand_ref[k * tile_count + 2 * r + 1] = jnp.where(left_rows, rolled, values)
        return carry

    lax.fori_loop(0, rows_per_block, build_rows, 0)
    chunk = 512
    for q in range(4):
        for r in range(atom_count // chunk):
            column = home_ref[r * chunk:(r + 1) * chunk, q:q + 1]
            spread_ref[q, r * chunk:(r + 1) * chunk, :] = jnp.broadcast_to(column, (chunk, LANES))
    acc_ref[...] = jnp.zeros(acc_ref.shape, jnp.float32)
    total = count_ref[0, 0]
    lane = lax.broadcasted_iota(jnp.int32, (1, LANES), 1)
    left = lane < TILE
    lane_full = lax.broadcasted_iota(jnp.int32, (TILE, LANES), 1)
    left_full = lane_full < TILE
    right_full = jnp.logical_not(left_full)
    diagonal = (lane_full % TILE) == lax.broadcasted_iota(jnp.int32, (TILE, LANES), 0)

    def pair_kernel(first):
        second = jnp.minimum(first + 1, pair_cap - 1)
        has_first = (first < total).astype(jnp.float32)
        has_second = (first + 1 < total).astype(jnp.float32)
        first = jnp.minimum(first, pair_cap - 1)
        home_a = jnp.clip(near_ref[0, 0, first], 0, tile_count - 1)
        cand_a = jnp.clip(far_ref[0, 0, first], 0, cand_tiles - 1)
        home_b = jnp.clip(near_ref[0, 0, second], 0, tile_count - 1)
        cand_b = jnp.clip(far_ref[0, 0, second], 0, cand_tiles - 1)
        rows = jnp.where(left, cand_ref[cand_a] * has_first, cand_ref[cand_b] * has_second)
        base_a = pl.multiple_of(home_a * TILE, TILE)
        base_b = pl.multiple_of(home_b * TILE, TILE)

        def near_q(q):
            return jnp.where(
                left, spread_ref[q, pl.ds(base_a, TILE), :], spread_ref[q, pl.ds(base_b, TILE), :]
            )

        delta_x = near_q(0) - rows[0:1]
        delta_y = near_q(1) - rows[1:2]
        delta_z = near_q(2) - rows[2:3]
        dist_sq = delta_x * delta_x + delta_y * delta_y + delta_z * delta_z
        shifted = dist_sq + soften * soften
        inv_spacing = lax.rsqrt(shifted)
        spacing = shifted * inv_spacing
        inv_width = lax.rsqrt(near_q(3) + rows[3:4])
        taper = jnp.maximum(1.0 - dist_sq * (1.0 / (cutoff * cutoff)), 0.0)
        kernel = lax.erf(inv_width * spacing) * inv_spacing * (taper * taper)
        self_half = jnp.where(
            left, (cand_a == home_a).astype(jnp.int32), (cand_b == home_b).astype(jnp.int32)
        )
        kernel = jnp.where(diagonal & (self_half > 0), 0.0, kernel)
        return kernel, rows, base_a, base_b

    def accumulate(kernel, rows, base_a, base_b):
        for c in range(2):
            contribution = kernel * rows[4 + c:5 + c]
            slot_a = acc_ref.at[c, pl.ds(base_a, TILE), :]
            pltpu.store(slot_a, slot_a[...] + contribution, mask=left_full)
            slot_b = acc_ref.at[c, pl.ds(base_b, TILE), :]
            pltpu.store(slot_b, slot_b[...] + contribution, mask=right_full)

    def body(k, carry):
        parts = [pair_kernel(16 * k + 2 * u) for u in range(8)]
        for part in parts:
            accumulate(*part)
        return carry

    lax.fori_loop(0, (total + 15) // 16, body, 0)
    ones = jnp.ones((8, LANES), jnp.float32)
    for c in range(2):
        summed = lax.dot_general(
            ones,
            acc_ref[c],
            (((1,), (1,)), ((), ())),
            precision=lax.Precision.HIGHEST,
            preferred_element_type=jnp.float32,
        )
        out_ref[c:c + 1, :] = summed[0:1]


def sweep(home_cols, blocks, near_list, far_list, pair_total):
    rows_per_block = blocks[0].shape[0]
    atom_count = rows_per_block * LANES
    smem = pl.BlockSpec(memory_space=pltpu.SMEM)
    vmem = pl.BlockSpec(memory_space=pltpu.VMEM)
    return pl.pallas_call(
        sweep_kernel,
        out_shape=jax.ShapeDtypeStruct((2, atom_count), jnp.float32),
        in_specs=[smem, smem, smem] + [vmem] * 6,
        out_specs=vmem,
        scratch_shapes=[
            pltpu.VMEM((10 * rows_per_block, 8, LANES), jnp.float32),
            pltpu.VMEM((4, atom_count, LANES), jnp.float32),
            pltpu.VMEM((2, atom_count, LANES), jnp.float32),
        ],
        compiler_params=pltpu.CompilerParams(vmem_limit_bytes=48 * 1024 * 1024),
    )(near_list, far_list, pair_total, home_cols, *blocks)


def on_device(
    positions,
    aux,
    aux_prev,
    resid,
    types,
    pair_tiles,
    pair_cands,
    pair_count,
    owner_tile,
    electroneg,
    hardness,
    widths,
):
    atom_count = aux.shape[-1]
    tile_count = atom_count // TILE
    type_row = types.reshape(atom_count)
    negativity = lookup(electroneg, type_row)
    hardness_row = lookup(hardness, type_row)
    radius = lookup(widths, type_row)
    charge_row = aux.reshape(atom_count)
    resid_row = resid.reshape(atom_count)
    packed = jnp.concatenate(
        [
            positions.reshape(3, atom_count),
            jnp.square(radius)[None],
            charge_row[None],
            resid_row[None],
            jnp.zeros((2, atom_count), jnp.float32),
        ],
        axis=0,
    )
    home_cols = packed.T
    packed = packed.reshape(8, atom_count // LANES, LANES).transpose(1, 0, 2)
    blocks = neighbours(packed)
    totals = sweep(home_cols, blocks, pair_tiles, pair_cands, pair_count)
    aux_field = totals[0].reshape(atom_count)
    resid_field = totals[1].reshape(atom_count)
    field = negativity + aux_field + resid_field
    planes = lax.axis_size("plane")
    devices = lax.axis_size("brick") * planes
    target = owner_tile.reshape(tile_count)
    plane_index = lax.axis_index("plane")

    def to_owners(rows):
        tiles = rows.reshape(rows.shape[0], tile_count, TILE)
        total = None
        for step in range(planes):
            owner = (plane_index + step) % planes
            local_target = target - owner * tile_count
            placer = (
                local_target[:, None] == jnp.arange(tile_count, dtype=jnp.int32)[None, :]
            ).astype(jnp.float32)
            part = jnp.einsum("ts,ctj->csj", placer, tiles, precision=lax.Precision.HIGHEST)
            if step:
                part = lax.ppermute(
                    part, "plane", [(i, (i + step) % planes) for i in range(planes)]
                )
            total = part if total is None else total + part
        return total

    local_sums = jnp.stack(
        [jnp.sum(charge_row), jnp.sum(field / hardness_row), jnp.sum(1.0 / hardness_row)]
    )
    sums_out = jnp.broadcast_to(jnp.pad(local_sums, (0, 5))[None, :], (devices, 8))
    sums_in = lax.all_to_all(sums_out, ("brick", "plane"), split_axis=0, concat_axis=0, tiled=True)
    placed = to_owners(jnp.stack([charge_row, hardness_row, field]))
    global_sums = jnp.sum(sums_in, axis=0)
    potential_level = (global_sums[0] + global_sums[1]) / global_sums[2]
    charges = (potential_level - field) / hardness_row
    placed_aux = placed[0]
    placed_charges = (potential_level - placed[2]) / placed[1]
    previous = aux_prev.reshape(tile_count, TILE)
    next_aux = 2.0 * placed_aux - previous + kappa * (placed_charges - placed_aux)
    return (charges.reshape(aux.shape), next_aux.reshape(aux.shape), resid_field.reshape(aux.shape))


def solution(mesh):
    in_specs = (
        P("brick", "plane", None, None),
        P("brick", "plane", None),
        P("brick", "plane", None),
        P("brick", "plane", None),
        P("brick", "plane", None),
        P("brick", "plane", None),
        P("brick", "plane", None),
        P("brick", "plane"),
        P("brick", "plane", None),
        P(),
        P(),
        P(),
    )
    out_specs = (P("brick", "plane", None), P("brick", "plane", None), P("brick", "plane", None))
    return jax.shard_map(
        on_device, mesh=mesh, in_specs=in_specs, out_specs=out_specs, check_vma=False
    )
```

```python
import numpy as np
import jax
import jax.numpy as jnp
from jax import lax
from jax.sharding import PartitionSpec as P
from jax.experimental import pallas as pl
from jax.experimental.pallas import tpu as pltpu

TX = 2
TY = 4
TILE = 64


cell_edge = 8.0
cutoff = 10.0
soften = 0.5
kappa = 1.86
pair_group = 256


def shifted_from(block, axis, step):
    count = lax.axis_size(axis)
    pairs = [(i, (i + step) % count) for i in range(count)]
    return lax.ppermute(block, axis, pairs)


def neighbours(block):
    return [
        block,
        shifted_from(block, "brick", 1),
        shifted_from(block, "brick", -1),
        shifted_from(block, "plane", 1),
        shifted_from(block, "plane", -1),
    ]


def lookup(type_table, type_row):
    chosen = (
        type_row[None, :] == jnp.arange(type_table.shape[0], dtype=jnp.int32)[:, None]
    ).astype(type_table.dtype)
    return jnp.sum(type_table[:, None] * chosen, axis=0)


def candidates(blocks, tile_count):
    joined = jnp.stack(blocks, axis=1)
    offsets = np.zeros((6, 5, 1), np.float32)
    offsets[0, 1] = -TX * cell_edge
    offsets[0, 2] = TX * cell_edge
    offsets[1, 3] = -TY * cell_edge
    offsets[1, 4] = TY * cell_edge
    joined = joined + offsets
    return joined.reshape(6, 5 * tile_count, TILE)


LANES = 128


def sweep_kernel(near_ref, far_ref, count_ref, home_ref, chi_ref, eta_ref, *refs):
    block_refs = refs[:5]
    out_ref, sum_ref, cand_ref, spread_ref, acc_ref = refs[5:]
    rows_per_block = block_refs[0].shape[0]
    atom_count = rows_per_block * LANES
    tile_count = atom_count // TILE
    cand_tiles = 5 * tile_count
    pair_cap = near_ref.shape[-1]
    sublane = lax.broadcasted_iota(jnp.int32, (8, LANES), 0)
    left_rows = lax.broadcasted_iota(jnp.int32, (8, LANES), 1) < TILE
    shifts = ((0.0, 0.0), (-TX * cell_edge, 0.0), (TX * cell_edge, 0.0),
              (0.0, -TY * cell_edge), (0.0, TY * cell_edge))

    def build_rows(r, carry):
        for k, (shift_x, shift_y) in enumerate(shifts):
            values = block_refs[k][r]
            if shift_x or shift_y:
                values = values + jnp.where(
                    sublane == 0, shift_x, jnp.where(sublane == 1, shift_y, 0.0)
                )
            rolled = pltpu.roll(values, TILE, 1)
            cand_ref[k * tile_count + 2 * r] = jnp.where(left_rows, values, rolled)
            cand_ref[k * tile_count + 2 * r + 1] = jnp.where(left_rows, rolled, values)
        return carry

    lax.fori_loop(0, rows_per_block, build_rows, 0)
    chunk = 512
    for q in range(4):
        for r in range(atom_count // chunk):
            column = home_ref[r * chunk:(r + 1) * chunk, q:q + 1]
            spread_ref[q, r * chunk:(r + 1) * chunk, :] = jnp.broadcast_to(column, (chunk, LANES))
    acc_ref[...] = jnp.zeros(acc_ref.shape, jnp.float32)
    total = count_ref[0, 0]
    lane = lax.broadcasted_iota(jnp.int32, (1, LANES), 1)
    left = lane < TILE
    lane_full = lax.broadcasted_iota(jnp.int32, (TILE, LANES), 1)
    left_full = lane_full < TILE
    right_full = jnp.logical_not(left_full)
    diagonal = (lane_full % TILE) == lax.broadcasted_iota(jnp.int32, (TILE, LANES), 0)

    def pair_kernel(first):
        second = jnp.minimum(first + 1, pair_cap - 1)
        has_first = (first < total).astype(jnp.float32)
        has_second = (first + 1 < total).astype(jnp.float32)
        first = jnp.minimum(first, pair_cap - 1)
        home_a = jnp.clip(near_ref[0, 0, first], 0, tile_count - 1)
        cand_a = jnp.clip(far_ref[0, 0, first], 0, cand_tiles - 1)
        home_b = jnp.clip(near_ref[0, 0, second], 0, tile_count - 1)
        cand_b = jnp.clip(far_ref[0, 0, second], 0, cand_tiles - 1)
        rows = jnp.where(left, cand_ref[cand_a] * has_first, cand_ref[cand_b] * has_second)
        base_a = pl.multiple_of(home_a * TILE, TILE)
        base_b = pl.multiple_of(home_b * TILE, TILE)

        def near_q(q):
            return jnp.where(
                left, spread_ref[q, pl.ds(base_a, TILE), :], spread_ref[q, pl.ds(base_b, TILE), :]
            )

        delta_x = near_q(0) - rows[0:1]
        delta_y = near_q(1) - rows[1:2]
        delta_z = near_q(2) - rows[2:3]
        dist_sq = delta_x * delta_x + delta_y * delta_y + delta_z * delta_z
        shifted = dist_sq + soften * soften
        inv_spacing = lax.rsqrt(shifted)
        spacing = shifted * inv_spacing
        inv_width = lax.rsqrt(near_q(3) + rows[3:4])
        taper = jnp.maximum(1.0 - dist_sq * (1.0 / (cutoff * cutoff)), 0.0)
        kernel = lax.erf(inv_width * spacing) * inv_spacing * (taper * taper)
        self_half = jnp.where(
            left, (cand_a == home_a).astype(jnp.int32), (cand_b == home_b).astype(jnp.int32)
        )
        kernel = jnp.where(diagonal & (self_half > 0), 0.0, kernel)
        return kernel, rows, base_a, base_b

    def accumulate(kernel, rows, base_a, base_b):
        for c in range(2):
            contribution = kernel * rows[4 + c:5 + c]
            slot_a = acc_ref.at[c, pl.ds(base_a, TILE), :]
            pltpu.store(slot_a, slot_a[...] + contribution, mask=left_full)
            slot_b = acc_ref.at[c, pl.ds(base_b, TILE), :]
            pltpu.store(slot_b, slot_b[...] + contribution, mask=right_full)

    def body(k, carry):
        parts = [pair_kernel(16 * k + 2 * u) for u in range(8)]
        for part in parts:
            accumulate(*part)
        return carry

    lax.fori_loop(0, (total + 15) // 16, body, 0)
    ones = jnp.ones((8, LANES), jnp.float32)
    fields = []
    for c in range(2):
        summed = lax.dot_general(
            ones,
            acc_ref[c],
            (((1,), (1,)), ((), ())),
            precision=lax.Precision.HIGHEST,
            preferred_element_type=jnp.float32,
        )
        fields.append(summed[0:1])
    field = chi_ref[...] + fields[0] + fields[1]
    out_ref[0:1, :] = field
    out_ref[1:2, :] = fields[1]
    sum_ref[...] = jnp.broadcast_to(jnp.sum(field / eta_ref[...]), sum_ref.shape)


def sweep(home_cols, chi, eta, blocks, near_list, far_list, pair_total):
    rows_per_block = blocks[0].shape[0]
    atom_count = rows_per_block * LANES
    smem = pl.BlockSpec(memory_space=pltpu.SMEM)
    vmem = pl.BlockSpec(memory_space=pltpu.VMEM)
    return pl.pallas_call(
        sweep_kernel,
        out_shape=(
            jax.ShapeDtypeStruct((2, atom_count), jnp.float32),
            jax.ShapeDtypeStruct((1, LANES), jnp.float32),
        ),
        in_specs=[smem, smem, smem] + [vmem] * 8,
        out_specs=(vmem, vmem),
        scratch_shapes=[
            pltpu.VMEM((10 * rows_per_block, 8, LANES), jnp.float32),
            pltpu.VMEM((4, atom_count, LANES), jnp.float32),
            pltpu.VMEM((2, atom_count, LANES), jnp.float32),
        ],
        compiler_params=pltpu.CompilerParams(vmem_limit_bytes=48 * 1024 * 1024),
    )(near_list, far_list, pair_total, home_cols, chi, eta, *blocks)


def on_device(
    positions,
    aux,
    aux_prev,
    resid,
    types,
    pair_tiles,
    pair_cands,
    pair_count,
    owner_tile,
    electroneg,
    hardness,
    widths,
):
    atom_count = aux.shape[-1]
    tile_count = atom_count // TILE
    type_row = types.reshape(atom_count)
    negativity = lookup(electroneg, type_row)
    hardness_row = lookup(hardness, type_row)
    radius = lookup(widths, type_row)
    charge_row = aux.reshape(atom_count)
    resid_row = resid.reshape(atom_count)
    packed = jnp.concatenate(
        [
            positions.reshape(3, atom_count),
            jnp.square(radius)[None],
            charge_row[None],
            resid_row[None],
            jnp.zeros((2, atom_count), jnp.float32),
        ],
        axis=0,
    )
    packed = packed.reshape(8, atom_count // LANES, LANES).transpose(1, 0, 2)
    home_cols = packed.transpose(0, 2, 1).reshape(atom_count, 8)
    blocks = neighbours(packed)
    totals, field_sum = sweep(
        home_cols,
        negativity[None],
        hardness_row[None],
        blocks,
        pair_tiles,
        pair_cands,
        pair_count,
    )
    field = totals[0]
    resid_field = totals[1]
    planes = lax.axis_size("plane")
    devices = lax.axis_size("brick") * planes
    target = owner_tile.reshape(tile_count)
    plane_index = lax.axis_index("plane")

    def to_owners(rows):
        tiles = rows.reshape(rows.shape[0], tile_count, TILE)
        total = None
        for step in range(planes):
            owner = (plane_index + step) % planes
            local_target = target - owner * tile_count
            placer = (
                local_target[:, None] == jnp.arange(tile_count, dtype=jnp.int32)[None, :]
            ).astype(jnp.float32)
            part = jnp.einsum("ts,ctj->csj", placer, tiles, precision=lax.Precision.HIGHEST)
            if step:
                part = lax.ppermute(
                    part, "plane", [(i, (i + step) % planes) for i in range(planes)]
                )
            total = part if total is None else total + part
        return total

    local_sums = jnp.stack(
        [jnp.sum(charge_row), field_sum[0, 0], jnp.sum(1.0 / hardness_row)]
    )
    sums_out = jnp.broadcast_to(jnp.pad(local_sums, (0, 5))[None, :], (devices, 8))
    sums_in = lax.all_to_all(sums_out, ("brick", "plane"), split_axis=0, concat_axis=0, tiled=True)
    placed = to_owners(jnp.stack([charge_row, hardness_row, field]))
    global_sums = jnp.sum(sums_in, axis=0)
    potential_level = (global_sums[0] + global_sums[1]) / global_sums[2]
    charges = (potential_level - field) / hardness_row
    placed_aux = placed[0]
    placed_charges = (potential_level - placed[2]) / placed[1]
    previous = aux_prev.reshape(tile_count, TILE)
    next_aux = 2.0 * placed_aux - previous + kappa * (placed_charges - placed_aux)
    return (charges.reshape(aux.shape), next_aux.reshape(aux.shape), resid_field.reshape(aux.shape))


def solution(mesh):
    in_specs = (
        P("brick", "plane", None, None),
        P("brick", "plane", None),
        P("brick", "plane", None),
        P("brick", "plane", None),
        P("brick", "plane", None),
        P("brick", "plane", None),
        P("brick", "plane", None),
        P("brick", "plane"),
        P("brick", "plane", None),
        P(),
        P(),
        P(),
    )
    out_specs = (P("brick", "plane", None), P("brick", "plane", None), P("brick", "plane", None))
    return jax.shard_map(
        on_device, mesh=mesh, in_specs=in_specs, out_specs=out_specs, check_vma=False
    )
```

```python
import numpy as np
import jax
import jax.numpy as jnp
from jax import lax
from jax.sharding import PartitionSpec as P
from jax.experimental import pallas as pl
from jax.experimental.pallas import tpu as pltpu

TX = 2
TY = 4
TILE = 64


cell_edge = 8.0
cutoff = 10.0
soften = 0.5
kappa = 1.86
pair_group = 256


def shifted_from(block, axis, step):
    count = lax.axis_size(axis)
    pairs = [(i, (i + step) % count) for i in range(count)]
    return lax.ppermute(block, axis, pairs)


def neighbours(block):
    return [
        block,
        shifted_from(block, "brick", 1),
        shifted_from(block, "brick", -1),
        shifted_from(block, "plane", 1),
        shifted_from(block, "plane", -1),
    ]


def lookup(type_table, type_row):
    chosen = (
        type_row[None, :] == jnp.arange(type_table.shape[0], dtype=jnp.int32)[:, None]
    ).astype(type_table.dtype)
    return jnp.sum(type_table[:, None] * chosen, axis=0)


def candidates(blocks, tile_count):
    joined = jnp.stack(blocks, axis=1)
    offsets = np.zeros((6, 5, 1), np.float32)
    offsets[0, 1] = -TX * cell_edge
    offsets[0, 2] = TX * cell_edge
    offsets[1, 3] = -TY * cell_edge
    offsets[1, 4] = TY * cell_edge
    joined = joined + offsets
    return joined.reshape(6, 5 * tile_count, TILE)


LANES = 128


def sweep_kernel(near_ref, far_ref, count_ref, home_ref, chi_ref, eta_ref, *refs):
    block_refs = refs[:5]
    out_ref, sum_ref, cand_ref, spread_ref, acc_ref = refs[5:]
    rows_per_block = block_refs[0].shape[0]
    atom_count = rows_per_block * LANES
    tile_count = atom_count // TILE
    cand_tiles = 5 * tile_count
    pair_cap = near_ref.shape[-1]
    sublane = lax.broadcasted_iota(jnp.int32, (8, LANES), 0)
    left_rows = lax.broadcasted_iota(jnp.int32, (8, LANES), 1) < TILE
    shifts = ((0.0, 0.0), (-TX * cell_edge, 0.0), (TX * cell_edge, 0.0),
              (0.0, -TY * cell_edge), (0.0, TY * cell_edge))

    def build_rows(r, carry):
        for k, (shift_x, shift_y) in enumerate(shifts):
            values = block_refs[k][r]
            if shift_x or shift_y:
                values = values + jnp.where(
                    sublane == 0, shift_x, jnp.where(sublane == 1, shift_y, 0.0)
                )
            rolled = pltpu.roll(values, TILE, 1)
            cand_ref[k * tile_count + 2 * r] = jnp.where(left_rows, values, rolled)
            cand_ref[k * tile_count + 2 * r + 1] = jnp.where(left_rows, rolled, values)
        return carry

    lax.fori_loop(0, rows_per_block, build_rows, 0)
    chunk = 512
    for q in range(4):
        for r in range(atom_count // chunk):
            column = home_ref[r * chunk:(r + 1) * chunk, q:q + 1]
            spread_ref[q, r * chunk:(r + 1) * chunk, :] = jnp.broadcast_to(column, (chunk, LANES))
    acc_ref[...] = jnp.zeros(acc_ref.shape, jnp.float32)
    total = count_ref[0, 0]
    lane = lax.broadcasted_iota(jnp.int32, (1, LANES), 1)
    left = lane < TILE
    lane_full = lax.broadcasted_iota(jnp.int32, (TILE, LANES), 1)
    left_full = lane_full < TILE
    right_full = jnp.logical_not(left_full)
    diagonal = (lane_full % TILE) == lax.broadcasted_iota(jnp.int32, (TILE, LANES), 0)

    def pair_kernel(first):
        second = jnp.minimum(first + 1, pair_cap - 1)
        has_first = (first < total).astype(jnp.float32)
        has_second = (first + 1 < total).astype(jnp.float32)
        first = jnp.minimum(first, pair_cap - 1)
        home_a = jnp.clip(near_ref[0, 0, first], 0, tile_count - 1)
        cand_a = jnp.clip(far_ref[0, 0, first], 0, cand_tiles - 1)
        home_b = jnp.clip(near_ref[0, 0, second], 0, tile_count - 1)
        cand_b = jnp.clip(far_ref[0, 0, second], 0, cand_tiles - 1)
        rows = jnp.where(left, cand_ref[cand_a] * has_first, cand_ref[cand_b] * has_second)
        base_a = pl.multiple_of(home_a * TILE, TILE)
        base_b = pl.multiple_of(home_b * TILE, TILE)

        def near_q(q):
            return jnp.where(
                left, spread_ref[q, pl.ds(base_a, TILE), :], spread_ref[q, pl.ds(base_b, TILE), :]
            )

        delta_x = near_q(0) - rows[0:1]
        delta_y = near_q(1) - rows[1:2]
        delta_z = near_q(2) - rows[2:3]
        dist_sq = delta_x * delta_x + delta_y * delta_y + delta_z * delta_z
        shifted = dist_sq + soften * soften
        inv_spacing = lax.rsqrt(shifted)
        spacing = shifted * inv_spacing
        inv_width = lax.rsqrt(near_q(3) + rows[3:4])
        taper = jnp.maximum(1.0 - dist_sq * (1.0 / (cutoff * cutoff)), 0.0)
        kernel = lax.erf(inv_width * spacing) * inv_spacing * (taper * taper)
        self_half = jnp.where(
            left, (cand_a == home_a).astype(jnp.int32), (cand_b == home_b).astype(jnp.int32)
        )
        kernel = jnp.where(diagonal & (self_half > 0), 0.0, kernel)
        return kernel, rows, base_a, base_b

    def accumulate(kernel, rows, base_a, base_b):
        for c in range(2):
            contribution = kernel * rows[4 + c:5 + c]
            slot_a = acc_ref.at[c, pl.ds(base_a, TILE), :]
            pltpu.store(slot_a, slot_a[...] + contribution, mask=left_full)
            slot_b = acc_ref.at[c, pl.ds(base_b, TILE), :]
            pltpu.store(slot_b, slot_b[...] + contribution, mask=right_full)

    def body(k, carry):
        parts = [pair_kernel(16 * k + 2 * u) for u in range(8)]
        for part in parts:
            accumulate(*part)
        return carry

    lax.fori_loop(0, (total + 15) // 16, body, 0)
    ones = jnp.ones((8, LANES), jnp.float32)
    fields = []
    for c in range(2):
        summed = lax.dot_general(
            ones,
            acc_ref[c],
            (((1,), (1,)), ((), ())),
            precision=lax.Precision.HIGH,
            preferred_element_type=jnp.float32,
        )
        fields.append(summed[0:1])
    field = chi_ref[...] + fields[0] + fields[1]
    out_ref[0:1, :] = field
    out_ref[1:2, :] = fields[1]
    sum_ref[...] = jnp.broadcast_to(jnp.sum(field / eta_ref[...]), sum_ref.shape)


def sweep(home_cols, chi, eta, blocks, near_list, far_list, pair_total):
    rows_per_block = blocks[0].shape[0]
    atom_count = rows_per_block * LANES
    smem = pl.BlockSpec(memory_space=pltpu.SMEM)
    vmem = pl.BlockSpec(memory_space=pltpu.VMEM)
    return pl.pallas_call(
        sweep_kernel,
        out_shape=(
            jax.ShapeDtypeStruct((2, atom_count), jnp.float32),
            jax.ShapeDtypeStruct((1, LANES), jnp.float32),
        ),
        in_specs=[smem, smem, smem] + [vmem] * 8,
        out_specs=(vmem, vmem),
        scratch_shapes=[
            pltpu.VMEM((10 * rows_per_block, 8, LANES), jnp.float32),
            pltpu.VMEM((4, atom_count, LANES), jnp.float32),
            pltpu.VMEM((2, atom_count, LANES), jnp.float32),
        ],
        compiler_params=pltpu.CompilerParams(vmem_limit_bytes=48 * 1024 * 1024),
    )(near_list, far_list, pair_total, home_cols, chi, eta, *blocks)


def on_device(
    positions,
    aux,
    aux_prev,
    resid,
    types,
    pair_tiles,
    pair_cands,
    pair_count,
    owner_tile,
    electroneg,
    hardness,
    widths,
):
    atom_count = aux.shape[-1]
    tile_count = atom_count // TILE
    type_row = types.reshape(atom_count)
    negativity = lookup(electroneg, type_row)
    hardness_row = lookup(hardness, type_row)
    radius = lookup(widths, type_row)
    charge_row = aux.reshape(atom_count)
    resid_row = resid.reshape(atom_count)
    packed = jnp.concatenate(
        [
            positions.reshape(3, atom_count),
            jnp.square(radius)[None],
            charge_row[None],
            resid_row[None],
            jnp.zeros((2, atom_count), jnp.float32),
        ],
        axis=0,
    )
    packed = packed.reshape(8, atom_count // LANES, LANES).transpose(1, 0, 2)
    home_cols = packed.transpose(0, 2, 1).reshape(atom_count, 8)
    blocks = neighbours(packed)
    totals, field_sum = sweep(
        home_cols,
        negativity[None],
        hardness_row[None],
        blocks,
        pair_tiles,
        pair_cands,
        pair_count,
    )
    field = totals[0]
    resid_field = totals[1]
    planes = lax.axis_size("plane")
    devices = lax.axis_size("brick") * planes
    target = owner_tile.reshape(tile_count)
    plane_index = lax.axis_index("plane")

    def to_owners(rows):
        tiles = rows.reshape(rows.shape[0], tile_count, TILE)
        total = None
        for step in range(planes):
            owner = (plane_index + step) % planes
            local_target = target - owner * tile_count
            placer = (
                local_target[:, None] == jnp.arange(tile_count, dtype=jnp.int32)[None, :]
            ).astype(jnp.float32)
            part = jnp.einsum("ts,ctj->csj", placer, tiles, precision=lax.Precision.HIGHEST)
            if step:
                part = lax.ppermute(
                    part, "plane", [(i, (i + step) % planes) for i in range(planes)]
                )
            total = part if total is None else total + part
        return total

    local_sums = jnp.stack(
        [jnp.sum(charge_row), field_sum[0, 0], jnp.sum(1.0 / hardness_row)]
    )
    sums_out = jnp.broadcast_to(jnp.pad(local_sums, (0, 5))[None, :], (devices, 8))
    sums_in = lax.all_to_all(sums_out, ("brick", "plane"), split_axis=0, concat_axis=0, tiled=True)
    placed = to_owners(jnp.stack([charge_row, hardness_row, field]))
    global_sums = jnp.sum(sums_in, axis=0)
    potential_level = (global_sums[0] + global_sums[1]) / global_sums[2]
    charges = (potential_level - field) / hardness_row
    placed_aux = placed[0]
    placed_charges = (potential_level - placed[2]) / placed[1]
    previous = aux_prev.reshape(tile_count, TILE)
    next_aux = 2.0 * placed_aux - previous + kappa * (placed_charges - placed_aux)
    return (charges.reshape(aux.shape), next_aux.reshape(aux.shape), resid_field.reshape(aux.shape))


def solution(mesh):
    in_specs = (
        P("brick", "plane", None, None),
        P("brick", "plane", None),
        P("brick", "plane", None),
        P("brick", "plane", None),
        P("brick", "plane", None),
        P("brick", "plane", None),
        P("brick", "plane", None),
        P("brick", "plane"),
        P("brick", "plane", None),
        P(),
        P(),
        P(),
    )
    out_specs = (P("brick", "plane", None), P("brick", "plane", None), P("brick", "plane", None))
    return jax.shard_map(
        on_device, mesh=mesh, in_specs=in_specs, out_specs=out_specs, check_vma=False
    )
```

```python
import numpy as np
import jax
import jax.numpy as jnp
from jax import lax
from jax.sharding import PartitionSpec as P
from jax.experimental import pallas as pl
from jax.experimental.pallas import tpu as pltpu

TX = 2
TY = 4
TILE = 64


cell_edge = 8.0
cutoff = 10.0
soften = 0.5
kappa = 1.86
pair_group = 256


def shifted_from(block, axis, step):
    count = lax.axis_size(axis)
    pairs = [(i, (i + step) % count) for i in range(count)]
    return lax.ppermute(block, axis, pairs)


def neighbours(block):
    return [
        block,
        shifted_from(block, "brick", 1),
        shifted_from(block, "brick", -1),
        shifted_from(block, "plane", 1),
        shifted_from(block, "plane", -1),
    ]


def lookup(type_table, type_row):
    chosen = (
        type_row[None, :] == jnp.arange(type_table.shape[0], dtype=jnp.int32)[:, None]
    ).astype(type_table.dtype)
    return jnp.sum(type_table[:, None] * chosen, axis=0)


def candidates(blocks, tile_count):
    joined = jnp.stack(blocks, axis=1)
    offsets = np.zeros((6, 5, 1), np.float32)
    offsets[0, 1] = -TX * cell_edge
    offsets[0, 2] = TX * cell_edge
    offsets[1, 3] = -TY * cell_edge
    offsets[1, 4] = TY * cell_edge
    joined = joined + offsets
    return joined.reshape(6, 5 * tile_count, TILE)


LANES = 128


def sweep_kernel(near_ref, far_ref, count_ref, home_ref, chi_ref, eta_ref, *refs):
    block_refs = refs[:5]
    out_ref, sum_ref, cand_ref, spread_ref, acc_ref = refs[5:]
    rows_per_block = block_refs[0].shape[0]
    atom_count = rows_per_block * LANES
    tile_count = atom_count // TILE
    cand_tiles = 5 * tile_count
    pair_cap = near_ref.shape[-1]
    sublane = lax.broadcasted_iota(jnp.int32, (8, LANES), 0)
    left_rows = lax.broadcasted_iota(jnp.int32, (8, LANES), 1) < TILE
    shifts = ((0.0, 0.0), (-TX * cell_edge, 0.0), (TX * cell_edge, 0.0),
              (0.0, -TY * cell_edge), (0.0, TY * cell_edge))

    def build_rows(r, carry):
        for k, (shift_x, shift_y) in enumerate(shifts):
            values = block_refs[k][r]
            if shift_x or shift_y:
                values = values + jnp.where(
                    sublane == 0, shift_x, jnp.where(sublane == 1, shift_y, 0.0)
                )
            rolled = pltpu.roll(values, TILE, 1)
            cand_ref[k * tile_count + 2 * r] = jnp.where(left_rows, values, rolled)
            cand_ref[k * tile_count + 2 * r + 1] = jnp.where(left_rows, rolled, values)
        return carry

    lax.fori_loop(0, rows_per_block, build_rows, 0)
    chunk = 512
    for q in range(4):
        for r in range(atom_count // chunk):
            column = home_ref[r * chunk:(r + 1) * chunk, q:q + 1]
            spread_ref[q, r * chunk:(r + 1) * chunk, :] = jnp.broadcast_to(column, (chunk, LANES))
    acc_ref[...] = jnp.zeros(acc_ref.shape, jnp.float32)
    total = count_ref[0, 0]
    lane = lax.broadcasted_iota(jnp.int32, (1, LANES), 1)
    left = lane < TILE
    lane_full = lax.broadcasted_iota(jnp.int32, (TILE, LANES), 1)
    left_full = lane_full < TILE
    right_full = jnp.logical_not(left_full)
    diagonal = (lane_full % TILE) == lax.broadcasted_iota(jnp.int32, (TILE, LANES), 0)

    def pair_kernel(first):
        second = jnp.minimum(first + 1, pair_cap - 1)
        has_first = (first < total).astype(jnp.float32)
        has_second = (first + 1 < total).astype(jnp.float32)
        first = jnp.minimum(first, pair_cap - 1)
        home_a = jnp.clip(near_ref[0, 0, first], 0, tile_count - 1)
        cand_a = jnp.clip(far_ref[0, 0, first], 0, cand_tiles - 1)
        home_b = jnp.clip(near_ref[0, 0, second], 0, tile_count - 1)
        cand_b = jnp.clip(far_ref[0, 0, second], 0, cand_tiles - 1)
        rows = jnp.where(left, cand_ref[cand_a] * has_first, cand_ref[cand_b] * has_second)
        base_a = pl.multiple_of(home_a * TILE, TILE)
        base_b = pl.multiple_of(home_b * TILE, TILE)

        def near_q(q):
            return jnp.where(
                left, spread_ref[q, pl.ds(base_a, TILE), :], spread_ref[q, pl.ds(base_b, TILE), :]
            )

        delta_x = near_q(0) - rows[0:1]
        delta_y = near_q(1) - rows[1:2]
        delta_z = near_q(2) - rows[2:3]
        dist_sq = delta_x * delta_x + delta_y * delta_y + delta_z * delta_z
        shifted = dist_sq + soften * soften
        inv_spacing = lax.rsqrt(shifted)
        spacing = shifted * inv_spacing
        inv_width = lax.rsqrt(near_q(3) + rows[3:4])
        taper = jnp.maximum(1.0 - dist_sq * (1.0 / (cutoff * cutoff)), 0.0)
        kernel = lax.erf(inv_width * spacing) * inv_spacing * (taper * taper)
        self_half = jnp.where(
            left, (cand_a == home_a).astype(jnp.int32), (cand_b == home_b).astype(jnp.int32)
        )
        kernel = jnp.where(diagonal & (self_half > 0), 0.0, kernel)
        return kernel, rows, base_a, base_b

    def accumulate(kernel, rows, base_a, base_b):
        for c in range(2):
            contribution = kernel * rows[4 + c:5 + c]
            slot_a = acc_ref.at[c, pl.ds(base_a, TILE), :]
            pltpu.store(slot_a, slot_a[...] + contribution, mask=left_full)
            slot_b = acc_ref.at[c, pl.ds(base_b, TILE), :]
            pltpu.store(slot_b, slot_b[...] + contribution, mask=right_full)

    def body(k, carry):
        parts = [pair_kernel(16 * k + 2 * u) for u in range(8)]
        for part in parts:
            accumulate(*part)
        return carry

    lax.fori_loop(0, (total + 15) // 16, body, 0)
    ones = jnp.ones((8, LANES), jnp.float32)
    fields = []
    for c in range(2):
        summed = lax.dot_general(
            ones,
            acc_ref[c],
            (((1,), (1,)), ((), ())),
            precision=lax.Precision.HIGH,
            preferred_element_type=jnp.float32,
        )
        fields.append(summed[0:1])
    field = chi_ref[...] + fields[0] + fields[1]
    out_ref[0:1, :] = field
    out_ref[1:2, :] = fields[1]
    eta = eta_ref[...]
    sums = (
        jnp.sum(block_refs[0][:, 4:5, :]),
        jnp.sum(field / eta),
        jnp.sum(1.0 / eta),
    )
    column = lax.broadcasted_iota(jnp.int32, sum_ref.shape, 1)
    sum_ref[...] = jnp.where(
        column == 0, sums[0], jnp.where(column == 1, sums[1], jnp.where(column == 2, sums[2], 0.0))
    )


def sweep(home_cols, chi, eta, blocks, near_list, far_list, pair_total, devices):
    rows_per_block = blocks[0].shape[0]
    atom_count = rows_per_block * LANES
    smem = pl.BlockSpec(memory_space=pltpu.SMEM)
    vmem = pl.BlockSpec(memory_space=pltpu.VMEM)
    return pl.pallas_call(
        sweep_kernel,
        out_shape=(
            jax.ShapeDtypeStruct((2, atom_count), jnp.float32),
            jax.ShapeDtypeStruct((devices, 8), jnp.float32),
        ),
        in_specs=[smem, smem, smem] + [vmem] * 8,
        out_specs=(vmem, vmem),
        scratch_shapes=[
            pltpu.VMEM((10 * rows_per_block, 8, LANES), jnp.float32),
            pltpu.VMEM((4, atom_count, LANES), jnp.float32),
            pltpu.VMEM((2, atom_count, LANES), jnp.float32),
        ],
        compiler_params=pltpu.CompilerParams(vmem_limit_bytes=48 * 1024 * 1024),
    )(near_list, far_list, pair_total, home_cols, chi, eta, *blocks)


def on_device(
    positions,
    aux,
    aux_prev,
    resid,
    types,
    pair_tiles,
    pair_cands,
    pair_count,
    owner_tile,
    electroneg,
    hardness,
    widths,
):
    atom_count = aux.shape[-1]
    tile_count = atom_count // TILE
    type_row = types.reshape(atom_count)
    negativity = lookup(electroneg, type_row)
    hardness_row = lookup(hardness, type_row)
    radius = lookup(widths, type_row)
    charge_row = aux.reshape(atom_count)
    resid_row = resid.reshape(atom_count)
    packed = jnp.concatenate(
        [
            positions.reshape(3, atom_count),
            jnp.square(radius)[None],
            charge_row[None],
            resid_row[None],
            jnp.zeros((2, atom_count), jnp.float32),
        ],
        axis=0,
    )
    packed = packed.reshape(8, atom_count // LANES, LANES).transpose(1, 0, 2)
    home_cols = packed.transpose(0, 2, 1).reshape(atom_count, 8)
    blocks = neighbours(packed)
    devices = lax.axis_size("brick") * lax.axis_size("plane")
    totals, sums_out = sweep(
        home_cols,
        negativity[None],
        hardness_row[None],
        blocks,
        pair_tiles,
        pair_cands,
        pair_count,
        devices,
    )
    field = totals[0]
    resid_field = totals[1]
    planes = lax.axis_size("plane")
    devices = lax.axis_size("brick") * planes
    target = owner_tile.reshape(tile_count)
    plane_index = lax.axis_index("plane")

    def to_owners(rows):
        tiles = rows.reshape(rows.shape[0], tile_count, TILE)
        total = None
        for step in range(planes):
            owner = (plane_index + step) % planes
            local_target = target - owner * tile_count
            placer = (
                local_target[:, None] == jnp.arange(tile_count, dtype=jnp.int32)[None, :]
            ).astype(jnp.float32)
            part = jnp.einsum("ts,ctj->csj", placer, tiles, precision=lax.Precision.HIGHEST)
            if step:
                part = lax.ppermute(
                    part, "plane", [(i, (i + step) % planes) for i in range(planes)]
                )
            total = part if total is None else total + part
        return total

    sums_in = lax.all_to_all(sums_out, ("brick", "plane"), split_axis=0, concat_axis=0, tiled=True)
    placed = to_owners(jnp.stack([charge_row, hardness_row, field]))
    global_sums = jnp.sum(sums_in, axis=0)
    potential_level = (global_sums[0] + global_sums[1]) / global_sums[2]
    charges = (potential_level - field) / hardness_row
    placed_aux = placed[0]
    placed_charges = (potential_level - placed[2]) / placed[1]
    previous = aux_prev.reshape(tile_count, TILE)
    next_aux = 2.0 * placed_aux - previous + kappa * (placed_charges - placed_aux)
    return (charges.reshape(aux.shape), next_aux.reshape(aux.shape), resid_field.reshape(aux.shape))


def solution(mesh):
    in_specs = (
        P("brick", "plane", None, None),
        P("brick", "plane", None),
        P("brick", "plane", None),
        P("brick", "plane", None),
        P("brick", "plane", None),
        P("brick", "plane", None),
        P("brick", "plane", None),
        P("brick", "plane"),
        P("brick", "plane", None),
        P(),
        P(),
        P(),
    )
    out_specs = (P("brick", "plane", None), P("brick", "plane", None), P("brick", "plane", None))
    return jax.shard_map(
        on_device, mesh=mesh, in_specs=in_specs, out_specs=out_specs, check_vma=False
    )
```

```python
import functools

import numpy as np
import jax
import jax.numpy as jnp
from jax import lax
from jax.sharding import PartitionSpec as P
from jax.experimental import pallas as pl
from jax.experimental.pallas import tpu as pltpu

TX = 2
TY = 4
TILE = 64


cell_edge = 8.0
cutoff = 10.0
soften = 0.5
kappa = 1.86
pair_group = 256


def shifted_from(block, axis, step):
    count = lax.axis_size(axis)
    pairs = [(i, (i + step) % count) for i in range(count)]
    return lax.ppermute(block, axis, pairs)


def neighbours(block):
    return [
        block,
        shifted_from(block, "brick", 1),
        shifted_from(block, "brick", -1),
        shifted_from(block, "plane", 1),
        shifted_from(block, "plane", -1),
    ]


def lookup(type_table, type_row):
    chosen = (
        type_row[None, :] == jnp.arange(type_table.shape[0], dtype=jnp.int32)[:, None]
    ).astype(type_table.dtype)
    return jnp.sum(type_table[:, None] * chosen, axis=0)


def candidates(blocks, tile_count):
    joined = jnp.stack(blocks, axis=1)
    offsets = np.zeros((6, 5, 1), np.float32)
    offsets[0, 1] = -TX * cell_edge
    offsets[0, 2] = TX * cell_edge
    offsets[1, 3] = -TY * cell_edge
    offsets[1, 4] = TY * cell_edge
    joined = joined + offsets
    return joined.reshape(6, 5 * tile_count, TILE)


LANES = 128
HELPER_SLACK = 320


def sweep_kernel(near_ref, far_ref, range_ref, home_ref, *refs, pair_cap, far_offset):
    block_refs = refs[:5]
    out_ref, cand_ref, spread_ref, acc_ref = refs[5:]
    rows_per_block = block_refs[0].shape[0]
    atom_count = rows_per_block * LANES
    tile_count = atom_count // TILE
    cand_tiles = 5 * tile_count
    sublane = lax.broadcasted_iota(jnp.int32, (8, LANES), 0)
    left_rows = lax.broadcasted_iota(jnp.int32, (8, LANES), 1) < TILE
    shifts = ((0.0, 0.0), (-TX * cell_edge, 0.0), (TX * cell_edge, 0.0),
              (0.0, -TY * cell_edge), (0.0, TY * cell_edge))

    def build_rows(r, carry):
        for k, (shift_x, shift_y) in enumerate(shifts):
            values = block_refs[k][r]
            if shift_x or shift_y:
                values = values + jnp.where(
                    sublane == 0, shift_x, jnp.where(sublane == 1, shift_y, 0.0)
                )
            rolled = pltpu.roll(values, TILE, 1)
            cand_ref[k * tile_count + 2 * r] = jnp.where(left_rows, values, rolled)
            cand_ref[k * tile_count + 2 * r + 1] = jnp.where(left_rows, rolled, values)
        return carry

    lax.fori_loop(0, rows_per_block, build_rows, 0)
    chunk = 512
    for q in range(4):
        for r in range(atom_count // chunk):
            column = home_ref[r * chunk:(r + 1) * chunk, q:q + 1]
            spread_ref[q, r * chunk:(r + 1) * chunk, :] = jnp.broadcast_to(column, (chunk, LANES))
    acc_ref[...] = jnp.zeros(acc_ref.shape, jnp.float32)
    begin = range_ref[0, 0]
    end = range_ref[0, 1]
    lane = lax.broadcasted_iota(jnp.int32, (1, LANES), 1)
    left = lane < TILE
    lane_full = lax.broadcasted_iota(jnp.int32, (TILE, LANES), 1)
    left_full = lane_full < TILE
    right_full = jnp.logical_not(left_full)
    diagonal = (lane_full % TILE) == lax.broadcasted_iota(jnp.int32, (TILE, LANES), 0)

    def pair_kernel(first):
        first = begin + first
        has_first = (first < end).astype(jnp.float32)
        has_second = (first + 1 < end).astype(jnp.float32)
        second = jnp.clip(first + 1, 0, pair_cap - 1)
        first = jnp.clip(first, 0, pair_cap - 1)
        home_a = jnp.clip(near_ref[0, 0, first], 0, tile_count - 1)
        cand_a = jnp.clip(far_ref[0, 0, far_offset + first], 0, cand_tiles - 1)
        home_b = jnp.clip(near_ref[0, 0, second], 0, tile_count - 1)
        cand_b = jnp.clip(far_ref[0, 0, far_offset + second], 0, cand_tiles - 1)
        rows = jnp.where(left, cand_ref[cand_a] * has_first, cand_ref[cand_b] * has_second)
        base_a = pl.multiple_of(home_a * TILE, TILE)
        base_b = pl.multiple_of(home_b * TILE, TILE)

        def near_q(q):
            return jnp.where(
                left, spread_ref[q, pl.ds(base_a, TILE), :], spread_ref[q, pl.ds(base_b, TILE), :]
            )

        delta_x = near_q(0) - rows[0:1]
        delta_y = near_q(1) - rows[1:2]
        delta_z = near_q(2) - rows[2:3]
        dist_sq = delta_x * delta_x + delta_y * delta_y + delta_z * delta_z
        shifted = dist_sq + soften * soften
        inv_spacing = lax.rsqrt(shifted)
        spacing = shifted * inv_spacing
        inv_width = lax.rsqrt(near_q(3) + rows[3:4])
        taper = jnp.maximum(1.0 - dist_sq * (1.0 / (cutoff * cutoff)), 0.0)
        kernel = lax.erf(inv_width * spacing) * inv_spacing * (taper * taper)
        self_half = jnp.where(
            left, (cand_a == home_a).astype(jnp.int32), (cand_b == home_b).astype(jnp.int32)
        )
        kernel = jnp.where(diagonal & (self_half > 0), 0.0, kernel)
        return kernel, rows, base_a, base_b

    def accumulate(kernel, rows, base_a, base_b):
        for c in range(2):
            contribution = kernel * rows[4 + c:5 + c]
            slot_a = acc_ref.at[c, pl.ds(base_a, TILE), :]
            pltpu.store(slot_a, slot_a[...] + contribution, mask=left_full)
            slot_b = acc_ref.at[c, pl.ds(base_b, TILE), :]
            pltpu.store(slot_b, slot_b[...] + contribution, mask=right_full)

    def body(k, carry):
        parts = [pair_kernel(16 * k + 2 * u) for u in range(8)]
        for part in parts:
            accumulate(*part)
        return carry

    lax.fori_loop(0, jnp.maximum(end - begin + 15, 0) // 16, body, 0)
    ones = jnp.ones((8, LANES), jnp.float32)
    for c in range(2):
        summed = lax.dot_general(
            ones,
            acc_ref[c],
            (((1,), (1,)), ((), ())),
            precision=lax.Precision.HIGH,
            preferred_element_type=jnp.float32,
        )
        out_ref[c:c + 1, :] = summed[0:1]


def sweep(home_cols, blocks, near_list, far_list, pair_range, far_offset):
    rows_per_block = blocks[0].shape[0]
    atom_count = rows_per_block * LANES
    smem = pl.BlockSpec(memory_space=pltpu.SMEM)
    vmem = pl.BlockSpec(memory_space=pltpu.VMEM)
    kernel = functools.partial(
        sweep_kernel, pair_cap=near_list.shape[-1], far_offset=far_offset
    )
    return pl.pallas_call(
        kernel,
        out_shape=jax.ShapeDtypeStruct((2, atom_count), jnp.float32),
        in_specs=[smem, smem, smem] + [vmem] * 6,
        out_specs=vmem,
        scratch_shapes=[
            pltpu.VMEM((10 * rows_per_block, 8, LANES), jnp.float32),
            pltpu.VMEM((4, atom_count, LANES), jnp.float32),
            pltpu.VMEM((2, atom_count, LANES), jnp.float32),
        ],
        compiler_params=pltpu.CompilerParams(vmem_limit_bytes=48 * 1024 * 1024),
    )(near_list, far_list, pair_range, home_cols, *blocks)


def on_device(
    positions,
    aux,
    aux_prev,
    resid,
    types,
    pair_tiles,
    pair_cands,
    pair_count,
    owner_tile,
    electroneg,
    hardness,
    widths,
):
    atom_count = aux.shape[-1]
    tile_count = atom_count // TILE
    type_row = types.reshape(atom_count)
    negativity = lookup(electroneg, type_row)
    hardness_row = lookup(hardness, type_row)
    radius = lookup(widths, type_row)
    charge_row = aux.reshape(atom_count)
    resid_row = resid.reshape(atom_count)
    packed = jnp.concatenate(
        [
            positions.reshape(3, atom_count),
            jnp.square(radius)[None],
            charge_row[None],
            resid_row[None],
            jnp.zeros((2, atom_count), jnp.float32),
        ],
        axis=0,
    )
    packed = packed.reshape(8, atom_count // LANES, LANES).transpose(1, 0, 2)
    home_cols = packed.transpose(0, 2, 1).reshape(atom_count, 8)
    blocks = neighbours(packed)
    pair_cap = pair_tiles.shape[-1]
    bricks = lax.axis_size("brick")
    partner = [(i, (i + bricks // 2) % bricks) for i in range(bricks)]
    lists = jnp.concatenate(
        [pair_tiles.reshape(-1), pair_cands.reshape(-1), pair_count.reshape(-1)]
    )
    partner_lists = lax.ppermute(lists, "brick", partner)
    partner_blocks = lax.ppermute(jnp.stack(blocks), "brick", partner)
    own_count = pair_count[0, 0]
    partner_count = partner_lists[2 * pair_cap]
    both = own_count + partner_count
    share = (both + HELPER_SLACK + 1) // 2
    own_keep = jnp.where(own_count > partner_count, jnp.minimum(own_count, share), own_count)
    partner_keep = jnp.where(
        partner_count > own_count, jnp.minimum(partner_count, share), partner_count
    )
    own_fields = sweep(
        home_cols,
        blocks,
        pair_tiles,
        pair_cands,
        jnp.stack([0, own_keep]).reshape(1, 2).astype(jnp.int32),
        0,
    )

    after_own = (0.0 * own_fields[0, 0]).astype(jnp.int32)

    def help_partner():
        partner_cols = partner_blocks[0].transpose(0, 2, 1).reshape(atom_count, 8)
        partner_list = partner_lists.reshape(1, 1, -1)
        return sweep(
            partner_cols,
            [partner_blocks[k] for k in range(5)],
            partner_list,
            partner_list,
            jnp.stack([partner_keep, partner_count]).reshape(1, 2).astype(jnp.int32) + after_own,
            pair_cap,
        )

    helped = lax.cond(
        partner_keep < partner_count,
        help_partner,
        lambda: jnp.zeros((2, atom_count), jnp.float32),
    )
    totals = own_fields + lax.ppermute(helped, "brick", partner)
    field = negativity + totals[0] + totals[1]
    resid_field = totals[1]
    planes = lax.axis_size("plane")
    devices = lax.axis_size("brick") * planes
    target = owner_tile.reshape(tile_count)
    plane_index = lax.axis_index("plane")

    def to_owners(rows):
        tiles = rows.reshape(rows.shape[0], tile_count, TILE)
        total = None
        for step in range(planes):
            owner = (plane_index + step) % planes
            local_target = target - owner * tile_count
            placer = (
                local_target[:, None] == jnp.arange(tile_count, dtype=jnp.int32)[None, :]
            ).astype(jnp.float32)
            part = jnp.einsum("ts,ctj->csj", placer, tiles, precision=lax.Precision.HIGHEST)
            if step:
                part = lax.ppermute(
                    part, "plane", [(i, (i + step) % planes) for i in range(planes)]
                )
            total = part if total is None else total + part
        return total

    local_sums = jnp.stack(
        [jnp.sum(charge_row), jnp.sum(field / hardness_row), jnp.sum(1.0 / hardness_row)]
    )
    sums_out = jnp.broadcast_to(jnp.pad(local_sums, (0, 5))[None, :], (devices, 8))
    sums_in = lax.all_to_all(sums_out, ("brick", "plane"), split_axis=0, concat_axis=0, tiled=True)
    placed = to_owners(jnp.stack([charge_row, hardness_row, field]))
    global_sums = jnp.sum(sums_in, axis=0)
    potential_level = (global_sums[0] + global_sums[1]) / global_sums[2]
    charges = (potential_level - field) / hardness_row
    placed_aux = placed[0]
    placed_charges = (potential_level - placed[2]) / placed[1]
    previous = aux_prev.reshape(tile_count, TILE)
    next_aux = 2.0 * placed_aux - previous + kappa * (placed_charges - placed_aux)
    return (charges.reshape(aux.shape), next_aux.reshape(aux.shape), resid_field.reshape(aux.shape))


def solution(mesh):
    in_specs = (
        P("brick", "plane", None, None),
        P("brick", "plane", None),
        P("brick", "plane", None),
        P("brick", "plane", None),
        P("brick", "plane", None),
        P("brick", "plane", None),
        P("brick", "plane", None),
        P("brick", "plane"),
        P("brick", "plane", None),
        P(),
        P(),
        P(),
    )
    out_specs = (P("brick", "plane", None), P("brick", "plane", None), P("brick", "plane", None))
    return jax.shard_map(
        on_device, mesh=mesh, in_specs=in_specs, out_specs=out_specs, check_vma=False
    )
```

```python
import functools

import numpy as np
import jax
import jax.numpy as jnp
from jax import lax
from jax.sharding import PartitionSpec as P
from jax.experimental import pallas as pl
from jax.experimental.pallas import tpu as pltpu

TX = 2
TY = 4
TILE = 64


cell_edge = 8.0
cutoff = 10.0
soften = 0.5
kappa = 1.86
pair_group = 256


def shifted_from(block, axis, step):
    count = lax.axis_size(axis)
    pairs = [(i, (i + step) % count) for i in range(count)]
    return lax.ppermute(block, axis, pairs)


def neighbours(block):
    return [
        block,
        shifted_from(block, "brick", 1),
        shifted_from(block, "brick", -1),
        shifted_from(block, "plane", 1),
        shifted_from(block, "plane", -1),
    ]


def lookup(type_table, type_row):
    chosen = (
        type_row[None, :] == jnp.arange(type_table.shape[0], dtype=jnp.int32)[:, None]
    ).astype(type_table.dtype)
    return jnp.sum(type_table[:, None] * chosen, axis=0)


def candidates(blocks, tile_count):
    joined = jnp.stack(blocks, axis=1)
    offsets = np.zeros((6, 5, 1), np.float32)
    offsets[0, 1] = -TX * cell_edge
    offsets[0, 2] = TX * cell_edge
    offsets[1, 3] = -TY * cell_edge
    offsets[1, 4] = TY * cell_edge
    joined = joined + offsets
    return joined.reshape(6, 5 * tile_count, TILE)


LANES = 128
OWN_SHARE = 1040


def sweep_kernel(near_ref, far_ref, range_ref, home_ref, *refs, pair_cap, far_offset):
    block_refs = refs[:5]
    out_ref, cand_ref, spread_ref, acc_ref = refs[5:]
    rows_per_block = block_refs[0].shape[0]
    atom_count = rows_per_block * LANES
    tile_count = atom_count // TILE
    cand_tiles = 5 * tile_count
    sublane = lax.broadcasted_iota(jnp.int32, (8, LANES), 0)
    left_rows = lax.broadcasted_iota(jnp.int32, (8, LANES), 1) < TILE
    shifts = ((0.0, 0.0), (-TX * cell_edge, 0.0), (TX * cell_edge, 0.0),
              (0.0, -TY * cell_edge), (0.0, TY * cell_edge))

    def build_rows(r, carry):
        for k, (shift_x, shift_y) in enumerate(shifts):
            values = block_refs[k][r]
            if shift_x or shift_y:
                values = values + jnp.where(
                    sublane == 0, shift_x, jnp.where(sublane == 1, shift_y, 0.0)
                )
            rolled = pltpu.roll(values, TILE, 1)
            cand_ref[k * tile_count + 2 * r] = jnp.where(left_rows, values, rolled)
            cand_ref[k * tile_count + 2 * r + 1] = jnp.where(left_rows, rolled, values)
        return carry

    lax.fori_loop(0, rows_per_block, build_rows, 0)
    chunk = 512
    for q in range(4):
        for r in range(atom_count // chunk):
            column = home_ref[r * chunk:(r + 1) * chunk, q:q + 1]
            spread_ref[q, r * chunk:(r + 1) * chunk, :] = jnp.broadcast_to(column, (chunk, LANES))
    acc_ref[...] = jnp.zeros(acc_ref.shape, jnp.float32)
    begin = range_ref[0, 0]
    end = range_ref[0, 1]
    lane = lax.broadcasted_iota(jnp.int32, (1, LANES), 1)
    left = lane < TILE
    lane_full = lax.broadcasted_iota(jnp.int32, (TILE, LANES), 1)
    left_full = lane_full < TILE
    right_full = jnp.logical_not(left_full)
    diagonal = (lane_full % TILE) == lax.broadcasted_iota(jnp.int32, (TILE, LANES), 0)

    def pair_kernel(first):
        first = begin + first
        has_first = (first < end).astype(jnp.float32)
        has_second = (first + 1 < end).astype(jnp.float32)
        second = jnp.clip(first + 1, 0, pair_cap - 1)
        first = jnp.clip(first, 0, pair_cap - 1)
        home_a = jnp.clip(near_ref[0, 0, first], 0, tile_count - 1)
        cand_a = jnp.clip(far_ref[0, 0, far_offset + first], 0, cand_tiles - 1)
        home_b = jnp.clip(near_ref[0, 0, second], 0, tile_count - 1)
        cand_b = jnp.clip(far_ref[0, 0, far_offset + second], 0, cand_tiles - 1)
        rows = jnp.where(left, cand_ref[cand_a] * has_first, cand_ref[cand_b] * has_second)
        base_a = pl.multiple_of(home_a * TILE, TILE)
        base_b = pl.multiple_of(home_b * TILE, TILE)

        def near_q(q):
            return jnp.where(
                left, spread_ref[q, pl.ds(base_a, TILE), :], spread_ref[q, pl.ds(base_b, TILE), :]
            )

        delta_x = near_q(0) - rows[0:1]
        delta_y = near_q(1) - rows[1:2]
        delta_z = near_q(2) - rows[2:3]
        dist_sq = delta_x * delta_x + delta_y * delta_y + delta_z * delta_z
        shifted = dist_sq + soften * soften
        inv_spacing = lax.rsqrt(shifted)
        spacing = shifted * inv_spacing
        inv_width = lax.rsqrt(near_q(3) + rows[3:4])
        taper = jnp.maximum(1.0 - dist_sq * (1.0 / (cutoff * cutoff)), 0.0)
        kernel = lax.erf(inv_width * spacing) * inv_spacing * (taper * taper)
        self_half = jnp.where(
            left, (cand_a == home_a).astype(jnp.int32), (cand_b == home_b).astype(jnp.int32)
        )
        kernel = jnp.where(diagonal & (self_half > 0), 0.0, kernel)
        return kernel, rows, base_a, base_b

    def accumulate(kernel, rows, base_a, base_b):
        for c in range(2):
            contribution = kernel * rows[4 + c:5 + c]
            slot_a = acc_ref.at[c, pl.ds(base_a, TILE), :]
            pltpu.store(slot_a, slot_a[...] + contribution, mask=left_full)
            slot_b = acc_ref.at[c, pl.ds(base_b, TILE), :]
            pltpu.store(slot_b, slot_b[...] + contribution, mask=right_full)

    def body(k, carry):
        parts = [pair_kernel(16 * k + 2 * u) for u in range(8)]
        for part in parts:
            accumulate(*part)
        return carry

    lax.fori_loop(0, jnp.maximum(end - begin + 15, 0) // 16, body, 0)
    ones = jnp.ones((8, LANES), jnp.float32)
    for c in range(2):
        summed = lax.dot_general(
            ones,
            acc_ref[c],
            (((1,), (1,)), ((), ())),
            precision=lax.Precision.HIGH,
            preferred_element_type=jnp.float32,
        )
        out_ref[c:c + 1, :] = summed[0:1]


def sweep(home_cols, blocks, near_list, far_list, pair_range, far_offset):
    rows_per_block = blocks[0].shape[0]
    atom_count = rows_per_block * LANES
    smem = pl.BlockSpec(memory_space=pltpu.SMEM)
    vmem = pl.BlockSpec(memory_space=pltpu.VMEM)
    kernel = functools.partial(
        sweep_kernel, pair_cap=near_list.shape[-1], far_offset=far_offset
    )
    return pl.pallas_call(
        kernel,
        out_shape=jax.ShapeDtypeStruct((2, atom_count), jnp.float32),
        in_specs=[smem, smem, smem] + [vmem] * 6,
        out_specs=vmem,
        scratch_shapes=[
            pltpu.VMEM((10 * rows_per_block, 8, LANES), jnp.float32),
            pltpu.VMEM((4, atom_count, LANES), jnp.float32),
            pltpu.VMEM((2, atom_count, LANES), jnp.float32),
        ],
        compiler_params=pltpu.CompilerParams(vmem_limit_bytes=48 * 1024 * 1024),
    )(near_list, far_list, pair_range, home_cols, *blocks)


def on_device(
    positions,
    aux,
    aux_prev,
    resid,
    types,
    pair_tiles,
    pair_cands,
    pair_count,
    owner_tile,
    electroneg,
    hardness,
    widths,
):
    atom_count = aux.shape[-1]
    tile_count = atom_count // TILE
    type_row = types.reshape(atom_count)
    negativity = lookup(electroneg, type_row)
    hardness_row = lookup(hardness, type_row)
    radius = lookup(widths, type_row)
    charge_row = aux.reshape(atom_count)
    resid_row = resid.reshape(atom_count)
    packed = jnp.concatenate(
        [
            positions.reshape(3, atom_count),
            jnp.square(radius)[None],
            charge_row[None],
            resid_row[None],
            jnp.zeros((2, atom_count), jnp.float32),
        ],
        axis=0,
    )
    packed = packed.reshape(8, atom_count // LANES, LANES).transpose(1, 0, 2)
    home_cols = packed.transpose(0, 2, 1).reshape(atom_count, 8)
    blocks = neighbours(packed)
    pair_cap = pair_tiles.shape[-1]
    bricks = lax.axis_size("brick")
    partner = [(i, (i + bricks // 2) % bricks) for i in range(bricks)]
    lists = jnp.concatenate(
        [pair_tiles.reshape(-1), pair_cands.reshape(-1), pair_count.reshape(-1)]
    )
    partner_lists = lax.ppermute(lists, "brick", partner)
    partner_blocks = lax.ppermute(jnp.stack(blocks), "brick", partner)
    own_count = pair_count[0, 0]
    own_keep = jnp.minimum(own_count, OWN_SHARE)
    own_fields = sweep(
        home_cols,
        blocks,
        pair_tiles,
        pair_cands,
        jnp.stack([0, own_keep]).reshape(1, 2).astype(jnp.int32),
        0,
    )

    after_own = (0.0 * own_fields[0, 0]).astype(jnp.int32)
    partner_lists = partner_lists + after_own
    partner_count = partner_lists[2 * pair_cap]
    partner_keep = jnp.minimum(partner_count, OWN_SHARE)

    def help_partner():
        partner_cols = partner_blocks[0].transpose(0, 2, 1).reshape(atom_count, 8)
        partner_list = partner_lists.reshape(1, 1, -1)
        return sweep(
            partner_cols,
            [partner_blocks[k] for k in range(5)],
            partner_list,
            partner_list,
            jnp.stack([partner_keep, partner_count]).reshape(1, 2).astype(jnp.int32) + after_own,
            pair_cap,
        )

    helped = lax.cond(
        partner_keep < partner_count,
        help_partner,
        lambda: jnp.zeros((2, atom_count), jnp.float32),
    )
    totals = own_fields + lax.ppermute(helped, "brick", partner)
    field = negativity + totals[0] + totals[1]
    resid_field = totals[1]
    planes = lax.axis_size("plane")
    devices = lax.axis_size("brick") * planes
    target = owner_tile.reshape(tile_count)
    plane_index = lax.axis_index("plane")

    def to_owners(rows):
        tiles = rows.reshape(rows.shape[0], tile_count, TILE)
        total = None
        for step in range(planes):
            owner = (plane_index + step) % planes
            local_target = target - owner * tile_count
            placer = (
                local_target[:, None] == jnp.arange(tile_count, dtype=jnp.int32)[None, :]
            ).astype(jnp.float32)
            part = jnp.einsum("ts,ctj->csj", placer, tiles, precision=lax.Precision.HIGHEST)
            if step:
                part = lax.ppermute(
                    part, "plane", [(i, (i + step) % planes) for i in range(planes)]
                )
            total = part if total is None else total + part
        return total

    local_sums = jnp.stack(
        [jnp.sum(charge_row), jnp.sum(field / hardness_row), jnp.sum(1.0 / hardness_row)]
    )
    sums_out = jnp.broadcast_to(jnp.pad(local_sums, (0, 5))[None, :], (devices, 8))
    sums_in = lax.all_to_all(sums_out, ("brick", "plane"), split_axis=0, concat_axis=0, tiled=True)
    placed = to_owners(jnp.stack([charge_row, hardness_row, field]))
    global_sums = jnp.sum(sums_in, axis=0)
    potential_level = (global_sums[0] + global_sums[1]) / global_sums[2]
    charges = (potential_level - field) / hardness_row
    placed_aux = placed[0]
    placed_charges = (potential_level - placed[2]) / placed[1]
    previous = aux_prev.reshape(tile_count, TILE)
    next_aux = 2.0 * placed_aux - previous + kappa * (placed_charges - placed_aux)
    return (charges.reshape(aux.shape), next_aux.reshape(aux.shape), resid_field.reshape(aux.shape))


def solution(mesh):
    in_specs = (
        P("brick", "plane", None, None),
        P("brick", "plane", None),
        P("brick", "plane", None),
        P("brick", "plane", None),
        P("brick", "plane", None),
        P("brick", "plane", None),
        P("brick", "plane", None),
        P("brick", "plane"),
        P("brick", "plane", None),
        P(),
        P(),
        P(),
    )
    out_specs = (P("brick", "plane", None), P("brick", "plane", None), P("brick", "plane", None))
    return jax.shard_map(
        on_device, mesh=mesh, in_specs=in_specs, out_specs=out_specs, check_vma=False
    )
```

```python
import numpy as np
import jax
import jax.numpy as jnp
from jax import lax
from jax.sharding import PartitionSpec as P
from jax.experimental import pallas as pl
from jax.experimental.pallas import tpu as pltpu

TX = 2
TY = 4
TILE = 64


cell_edge = 8.0
cutoff = 10.0
soften = 0.5
kappa = 1.86
pair_group = 256


def shifted_from(block, axis, step):
    count = lax.axis_size(axis)
    pairs = [(i, (i + step) % count) for i in range(count)]
    return lax.ppermute(block, axis, pairs)


def neighbours(block):
    return [
        block,
        shifted_from(block, "brick", 1),
        shifted_from(block, "brick", -1),
        shifted_from(block, "plane", 1),
        shifted_from(block, "plane", -1),
    ]


def lookup(type_table, type_row):
    chosen = (
        type_row[None, :] == jnp.arange(type_table.shape[0], dtype=jnp.int32)[:, None]
    ).astype(type_table.dtype)
    return jnp.sum(type_table[:, None] * chosen, axis=0)


def candidates(blocks, tile_count):
    joined = jnp.stack(blocks, axis=1)
    offsets = np.zeros((6, 5, 1), np.float32)
    offsets[0, 1] = -TX * cell_edge
    offsets[0, 2] = TX * cell_edge
    offsets[1, 3] = -TY * cell_edge
    offsets[1, 4] = TY * cell_edge
    joined = joined + offsets
    return joined.reshape(6, 5 * tile_count, TILE)


LANES = 128


def sweep_kernel(near_ref, far_ref, count_ref, home_ref, chi_ref, eta_ref, *refs):
    block_refs = refs[:5]
    out_ref, sum_ref, cand_ref, spread_ref, acc_ref = refs[5:]
    rows_per_block = block_refs[0].shape[0]
    atom_count = rows_per_block * LANES
    tile_count = atom_count // TILE
    cand_tiles = 5 * tile_count
    pair_cap = near_ref.shape[-1]
    sublane = lax.broadcasted_iota(jnp.int32, (8, LANES), 0)
    left_rows = lax.broadcasted_iota(jnp.int32, (8, LANES), 1) < TILE
    shifts = ((0.0, 0.0), (-TX * cell_edge, 0.0), (TX * cell_edge, 0.0),
              (0.0, -TY * cell_edge), (0.0, TY * cell_edge))

    def build_rows(r, carry):
        for k, (shift_x, shift_y) in enumerate(shifts):
            values = block_refs[k][r]
            if shift_x or shift_y:
                values = values + jnp.where(
                    sublane == 0, shift_x, jnp.where(sublane == 1, shift_y, 0.0)
                )
            rolled = pltpu.roll(values, TILE, 1)
            cand_ref[k * tile_count + 2 * r] = jnp.where(left_rows, values, rolled)
            cand_ref[k * tile_count + 2 * r + 1] = jnp.where(left_rows, rolled, values)
        return carry

    lax.fori_loop(0, rows_per_block, build_rows, 0)
    chunk = 512
    for q in range(4):
        for r in range(atom_count // chunk):
            column = home_ref[r * chunk:(r + 1) * chunk, q:q + 1]
            spread_ref[q, r * chunk:(r + 1) * chunk, :] = jnp.broadcast_to(column, (chunk, LANES))
    acc_ref[...] = jnp.zeros(acc_ref.shape, jnp.float32)
    total = count_ref[0, 0]
    lane = lax.broadcasted_iota(jnp.int32, (1, LANES), 1)
    left = lane < TILE
    lane_full = lax.broadcasted_iota(jnp.int32, (TILE, LANES), 1)
    left_full = lane_full < TILE
    right_full = jnp.logical_not(left_full)
    diagonal = (lane_full % TILE) == lax.broadcasted_iota(jnp.int32, (TILE, LANES), 0)

    def pair_kernel(first):
        second = jnp.minimum(first + 1, pair_cap - 1)
        has_first = (first < total).astype(jnp.float32)
        has_second = (first + 1 < total).astype(jnp.float32)
        first = jnp.minimum(first, pair_cap - 1)
        home_a = jnp.clip(near_ref[0, 0, first], 0, tile_count - 1)
        cand_a = jnp.clip(far_ref[0, 0, first], 0, cand_tiles - 1)
        home_b = jnp.clip(near_ref[0, 0, second], 0, tile_count - 1)
        cand_b = jnp.clip(far_ref[0, 0, second], 0, cand_tiles - 1)
        rows = jnp.where(left, cand_ref[cand_a] * has_first, cand_ref[cand_b] * has_second)
        base_a = pl.multiple_of(home_a * TILE, TILE)
        base_b = pl.multiple_of(home_b * TILE, TILE)

        def near_q(q):
            return jnp.where(
                left, spread_ref[q, pl.ds(base_a, TILE), :], spread_ref[q, pl.ds(base_b, TILE), :]
            )

        delta_x = near_q(0) - rows[0:1]
        delta_y = near_q(1) - rows[1:2]
        delta_z = near_q(2) - rows[2:3]
        dist_sq = delta_x * delta_x + delta_y * delta_y + delta_z * delta_z
        shifted = dist_sq + soften * soften
        inv_spacing = lax.rsqrt(shifted)
        spacing = shifted * inv_spacing
        inv_width = lax.rsqrt(near_q(3) + rows[3:4])
        taper = jnp.maximum(cutoff * cutoff - dist_sq, 0.0)
        kernel = lax.erf(inv_width * spacing) * inv_spacing * (taper * taper)
        self_half = jnp.where(
            left, (cand_a == home_a).astype(jnp.int32), (cand_b == home_b).astype(jnp.int32)
        )
        kernel = jnp.where(diagonal & (self_half > 0), 0.0, kernel)
        return kernel, rows, base_a, base_b

    def accumulate(kernel, rows, base_a, base_b):
        charges = rows[4:6] * (1.0 / (cutoff * cutoff)) ** 2
        for c in range(2):
            contribution = kernel * charges[c:c + 1]
            slot_a = acc_ref.at[c, pl.ds(base_a, TILE), :]
            pltpu.store(slot_a, slot_a[...] + contribution, mask=left_full)
            slot_b = acc_ref.at[c, pl.ds(base_b, TILE), :]
            pltpu.store(slot_b, slot_b[...] + contribution, mask=right_full)

    def body(k, carry):
        parts = [pair_kernel(24 * k + 2 * u) for u in range(12)]
        for part in parts:
            accumulate(*part)
        return carry

    lax.fori_loop(0, (total + 23) // 24, body, 0)
    ones = jnp.ones((8, LANES), jnp.float32)
    fields = []
    for c in range(2):
        summed = lax.dot_general(
            ones,
            acc_ref[c],
            (((1,), (1,)), ((), ())),
            precision=lax.Precision.HIGH,
            preferred_element_type=jnp.float32,
        )
        fields.append(summed[0:1])
    field = chi_ref[...] + fields[0] + fields[1]
    out_ref[0:1, :] = field
    out_ref[1:2, :] = fields[1]
    eta = eta_ref[...]
    sums = (
        jnp.sum(block_refs[0][:, 4:5, :]),
        jnp.sum(field / eta),
        jnp.sum(1.0 / eta),
    )
    column = lax.broadcasted_iota(jnp.int32, sum_ref.shape, 1)
    sum_ref[...] = jnp.where(
        column == 0, sums[0], jnp.where(column == 1, sums[1], jnp.where(column == 2, sums[2], 0.0))
    )


def sweep(home_cols, chi, eta, blocks, near_list, far_list, pair_total, devices):
    rows_per_block = blocks[0].shape[0]
    atom_count = rows_per_block * LANES
    smem = pl.BlockSpec(memory_space=pltpu.SMEM)
    vmem = pl.BlockSpec(memory_space=pltpu.VMEM)
    return pl.pallas_call(
        sweep_kernel,
        out_shape=(
            jax.ShapeDtypeStruct((2, atom_count), jnp.float32),
            jax.ShapeDtypeStruct((devices, 8), jnp.float32),
        ),
        in_specs=[smem, smem, smem] + [vmem] * 8,
        out_specs=(vmem, vmem),
        scratch_shapes=[
            pltpu.VMEM((10 * rows_per_block, 8, LANES), jnp.float32),
            pltpu.VMEM((4, atom_count, LANES), jnp.float32),
            pltpu.VMEM((2, atom_count, LANES), jnp.float32),
        ],
        compiler_params=pltpu.CompilerParams(vmem_limit_bytes=48 * 1024 * 1024),
    )(near_list, far_list, pair_total, home_cols, chi, eta, *blocks)


def on_device(
    positions,
    aux,
    aux_prev,
    resid,
    types,
    pair_tiles,
    pair_cands,
    pair_count,
    owner_tile,
    electroneg,
    hardness,
    widths,
):
    atom_count = aux.shape[-1]
    tile_count = atom_count // TILE
    type_row = types.reshape(atom_count)
    negativity = lookup(electroneg, type_row)
    hardness_row = lookup(hardness, type_row)
    radius = lookup(widths, type_row)
    charge_row = aux.reshape(atom_count)
    resid_row = resid.reshape(atom_count)
    packed = jnp.concatenate(
        [
            positions.reshape(3, atom_count),
            jnp.square(radius)[None],
            charge_row[None],
            resid_row[None],
            jnp.zeros((2, atom_count), jnp.float32),
        ],
        axis=0,
    )
    packed = packed.reshape(8, atom_count // LANES, LANES).transpose(1, 0, 2)
    home_cols = packed.transpose(0, 2, 1).reshape(atom_count, 8)
    blocks = neighbours(packed)
    devices = lax.axis_size("brick") * lax.axis_size("plane")
    totals, sums_out = sweep(
        home_cols,
        negativity[None],
        hardness_row[None],
        blocks,
        pair_tiles,
        pair_cands,
        pair_count,
        devices,
    )
    field = totals[0]
    resid_field = totals[1]
    planes = lax.axis_size("plane")
    devices = lax.axis_size("brick") * planes
    target = owner_tile.reshape(tile_count)
    plane_index = lax.axis_index("plane")

    def to_owners(rows):
        tiles = rows.reshape(rows.shape[0], tile_count, TILE)
        total = None
        for step in range(planes):
            owner = (plane_index + step) % planes
            local_target = target - owner * tile_count
            placer = (
                local_target[:, None] == jnp.arange(tile_count, dtype=jnp.int32)[None, :]
            ).astype(jnp.float32)
            part = jnp.einsum("ts,ctj->csj", placer, tiles, precision=lax.Precision.HIGHEST)
            if step:
                part = lax.ppermute(
                    part, "plane", [(i, (i + step) % planes) for i in range(planes)]
                )
            total = part if total is None else total + part
        return total

    sums_in = lax.all_to_all(sums_out, ("brick", "plane"), split_axis=0, concat_axis=0, tiled=True)
    placed = to_owners(jnp.stack([charge_row, hardness_row, field]))
    global_sums = jnp.sum(sums_in, axis=0)
    potential_level = (global_sums[0] + global_sums[1]) / global_sums[2]
    charges = (potential_level - field) / hardness_row
    placed_aux = placed[0]
    placed_charges = (potential_level - placed[2]) / placed[1]
    previous = aux_prev.reshape(tile_count, TILE)
    next_aux = 2.0 * placed_aux - previous + kappa * (placed_charges - placed_aux)
    return (charges.reshape(aux.shape), next_aux.reshape(aux.shape), resid_field.reshape(aux.shape))


def solution(mesh):
    in_specs = (
        P("brick", "plane", None, None),
        P("brick", "plane", None),
        P("brick", "plane", None),
        P("brick", "plane", None),
        P("brick", "plane", None),
        P("brick", "plane", None),
        P("brick", "plane", None),
        P("brick", "plane"),
        P("brick", "plane", None),
        P(),
        P(),
        P(),
    )
    out_specs = (P("brick", "plane", None), P("brick", "plane", None), P("brick", "plane", None))
    return jax.shard_map(
        on_device, mesh=mesh, in_specs=in_specs, out_specs=out_specs, check_vma=False
    )
```

```python
import numpy as np
import jax
import jax.numpy as jnp
from jax import lax
from jax.sharding import PartitionSpec as P
from jax.experimental import pallas as pl
from jax.experimental.pallas import tpu as pltpu

TX = 2
TY = 4
TILE = 64


cell_edge = 8.0
cutoff = 10.0
soften = 0.5
kappa = 1.86
pair_group = 256


def shifted_from(block, axis, step):
    count = lax.axis_size(axis)
    pairs = [(i, (i + step) % count) for i in range(count)]
    return lax.ppermute(block, axis, pairs)


def neighbours(block):
    return [
        block,
        shifted_from(block, "brick", 1),
        shifted_from(block, "brick", -1),
        shifted_from(block, "plane", 1),
        shifted_from(block, "plane", -1),
    ]


def lookup(type_table, type_row):
    chosen = (
        type_row[None, :] == jnp.arange(type_table.shape[0], dtype=jnp.int32)[:, None]
    ).astype(type_table.dtype)
    return jnp.sum(type_table[:, None] * chosen, axis=0)


def candidates(blocks, tile_count):
    joined = jnp.stack(blocks, axis=1)
    offsets = np.zeros((6, 5, 1), np.float32)
    offsets[0, 1] = -TX * cell_edge
    offsets[0, 2] = TX * cell_edge
    offsets[1, 3] = -TY * cell_edge
    offsets[1, 4] = TY * cell_edge
    joined = joined + offsets
    return joined.reshape(6, 5 * tile_count, TILE)


LANES = 128


def sweep_kernel(near_ref, far_ref, count_ref, home_ref, chi_ref, eta_ref, *refs):
    block_refs = refs[:5]
    out_ref, sum_ref, cand_ref, spread_ref, acc_ref = refs[5:]
    rows_per_block = block_refs[0].shape[0]
    atom_count = rows_per_block * LANES
    tile_count = atom_count // TILE
    cand_tiles = 5 * tile_count
    pair_cap = near_ref.shape[-1]
    sublane = lax.broadcasted_iota(jnp.int32, (8, LANES), 0)
    left_rows = lax.broadcasted_iota(jnp.int32, (8, LANES), 1) < TILE
    shifts = ((0.0, 0.0), (-TX * cell_edge, 0.0), (TX * cell_edge, 0.0),
              (0.0, -TY * cell_edge), (0.0, TY * cell_edge))

    def build_rows(r, carry):
        for k, (shift_x, shift_y) in enumerate(shifts):
            values = block_refs[k][r]
            if shift_x or shift_y:
                values = values + jnp.where(
                    sublane == 0, shift_x, jnp.where(sublane == 1, shift_y, 0.0)
                )
            rolled = pltpu.roll(values, TILE, 1)
            cand_ref[k * tile_count + 2 * r] = jnp.where(left_rows, values, rolled)
            cand_ref[k * tile_count + 2 * r + 1] = jnp.where(left_rows, rolled, values)
        return carry

    lax.fori_loop(0, rows_per_block, build_rows, 0)
    chunk = 512
    for q in range(4):
        for r in range(atom_count // chunk):
            column = home_ref[r * chunk:(r + 1) * chunk, q:q + 1]
            spread_ref[q, r * chunk:(r + 1) * chunk, :] = jnp.broadcast_to(column, (chunk, LANES))
    acc_ref[...] = jnp.zeros(acc_ref.shape, jnp.float32)
    total = count_ref[0, 0]
    lane = lax.broadcasted_iota(jnp.int32, (1, LANES), 1)
    left = lane < TILE
    lane_full = lax.broadcasted_iota(jnp.int32, (TILE, LANES), 1)
    left_full = lane_full < TILE
    right_full = jnp.logical_not(left_full)
    diagonal = (lane_full % TILE) == lax.broadcasted_iota(jnp.int32, (TILE, LANES), 0)

    def pair_kernel(first):
        second = jnp.minimum(first + 1, pair_cap - 1)
        has_first = (first < total).astype(jnp.float32)
        has_second = (first + 1 < total).astype(jnp.float32)
        first = jnp.minimum(first, pair_cap - 1)
        home_a = jnp.clip(near_ref[0, 0, first], 0, tile_count - 1)
        cand_a = jnp.clip(far_ref[0, 0, first], 0, cand_tiles - 1)
        home_b = jnp.clip(near_ref[0, 0, second], 0, tile_count - 1)
        cand_b = jnp.clip(far_ref[0, 0, second], 0, cand_tiles - 1)
        rows = jnp.where(left, cand_ref[cand_a] * has_first, cand_ref[cand_b] * has_second)
        base_a = pl.multiple_of(home_a * TILE, TILE)
        base_b = pl.multiple_of(home_b * TILE, TILE)

        def near_q(q):
            return jnp.where(
                left, spread_ref[q, pl.ds(base_a, TILE), :], spread_ref[q, pl.ds(base_b, TILE), :]
            )

        delta_x = near_q(0) - rows[0:1]
        delta_y = near_q(1) - rows[1:2]
        delta_z = near_q(2) - rows[2:3]
        dist_sq = delta_x * delta_x + delta_y * delta_y + delta_z * delta_z
        shifted = dist_sq + soften * soften
        inv_spacing = lax.rsqrt(shifted)
        spacing = shifted * inv_spacing
        inv_width = lax.rsqrt(near_q(3) + rows[3:4])
        taper = jnp.maximum(cutoff * cutoff - dist_sq, 0.0)
        kernel = lax.erf(inv_width * spacing) * inv_spacing * (taper * taper)
        self_half = jnp.where(
            left, (cand_a == home_a).astype(jnp.int32), (cand_b == home_b).astype(jnp.int32)
        )
        kernel = jnp.where(diagonal & (self_half > 0), 0.0, kernel)
        return kernel, rows, base_a, base_b

    def accumulate(kernel, rows, base_a, base_b):
        charges = rows[4:6] * (1.0 / (cutoff * cutoff)) ** 2
        for c in range(2):
            contribution = kernel * charges[c:c + 1]
            slot_a = acc_ref.at[c, pl.ds(base_a, TILE), :]
            pltpu.store(slot_a, slot_a[...] + contribution, mask=left_full)
            slot_b = acc_ref.at[c, pl.ds(base_b, TILE), :]
            pltpu.store(slot_b, slot_b[...] + contribution, mask=right_full)

    def body(k, carry):
        parts = [pair_kernel(32 * k + 2 * u) for u in range(16)]
        for part in parts:
            accumulate(*part)
        return carry

    lax.fori_loop(0, (total + 31) // 32, body, 0)
    ones = jnp.ones((8, LANES), jnp.float32)
    fields = []
    for c in range(2):
        summed = lax.dot_general(
            ones,
            acc_ref[c],
            (((1,), (1,)), ((), ())),
            precision=lax.Precision.HIGH,
            preferred_element_type=jnp.float32,
        )
        fields.append(summed[0:1])
    field = chi_ref[...] + fields[0] + fields[1]
    out_ref[0:1, :] = field
    out_ref[1:2, :] = fields[1]
    eta = eta_ref[...]
    sums = (
        jnp.sum(block_refs[0][:, 4:5, :]),
        jnp.sum(field / eta),
        jnp.sum(1.0 / eta),
    )
    column = lax.broadcasted_iota(jnp.int32, sum_ref.shape, 1)
    sum_ref[...] = jnp.where(
        column == 0, sums[0], jnp.where(column == 1, sums[1], jnp.where(column == 2, sums[2], 0.0))
    )


def sweep(home_cols, chi, eta, blocks, near_list, far_list, pair_total, devices):
    rows_per_block = blocks[0].shape[0]
    atom_count = rows_per_block * LANES
    smem = pl.BlockSpec(memory_space=pltpu.SMEM)
    vmem = pl.BlockSpec(memory_space=pltpu.VMEM)
    return pl.pallas_call(
        sweep_kernel,
        out_shape=(
            jax.ShapeDtypeStruct((2, atom_count), jnp.float32),
            jax.ShapeDtypeStruct((devices, 8), jnp.float32),
        ),
        in_specs=[smem, smem, smem] + [vmem] * 8,
        out_specs=(vmem, vmem),
        scratch_shapes=[
            pltpu.VMEM((10 * rows_per_block, 8, LANES), jnp.float32),
            pltpu.VMEM((4, atom_count, LANES), jnp.float32),
            pltpu.VMEM((2, atom_count, LANES), jnp.float32),
        ],
        compiler_params=pltpu.CompilerParams(vmem_limit_bytes=48 * 1024 * 1024),
    )(near_list, far_list, pair_total, home_cols, chi, eta, *blocks)


def on_device(
    positions,
    aux,
    aux_prev,
    resid,
    types,
    pair_tiles,
    pair_cands,
    pair_count,
    owner_tile,
    electroneg,
    hardness,
    widths,
):
    atom_count = aux.shape[-1]
    tile_count = atom_count // TILE
    type_row = types.reshape(atom_count)
    negativity = lookup(electroneg, type_row)
    hardness_row = lookup(hardness, type_row)
    radius = lookup(widths, type_row)
    charge_row = aux.reshape(atom_count)
    resid_row = resid.reshape(atom_count)
    packed = jnp.concatenate(
        [
            positions.reshape(3, atom_count),
            jnp.square(radius)[None],
            charge_row[None],
            resid_row[None],
            jnp.zeros((2, atom_count), jnp.float32),
        ],
        axis=0,
    )
    packed = packed.reshape(8, atom_count // LANES, LANES).transpose(1, 0, 2)
    home_cols = packed.transpose(0, 2, 1).reshape(atom_count, 8)
    blocks = neighbours(packed)
    devices = lax.axis_size("brick") * lax.axis_size("plane")
    totals, sums_out = sweep(
        home_cols,
        negativity[None],
        hardness_row[None],
        blocks,
        pair_tiles,
        pair_cands,
        pair_count,
        devices,
    )
    field = totals[0]
    resid_field = totals[1]
    planes = lax.axis_size("plane")
    devices = lax.axis_size("brick") * planes
    target = owner_tile.reshape(tile_count)
    plane_index = lax.axis_index("plane")

    def to_owners(rows):
        tiles = rows.reshape(rows.shape[0], tile_count, TILE)
        total = None
        for step in range(planes):
            owner = (plane_index + step) % planes
            local_target = target - owner * tile_count
            placer = (
                local_target[:, None] == jnp.arange(tile_count, dtype=jnp.int32)[None, :]
            ).astype(jnp.float32)
            part = jnp.einsum("ts,ctj->csj", placer, tiles, precision=lax.Precision.HIGHEST)
            if step:
                part = lax.ppermute(
                    part, "plane", [(i, (i + step) % planes) for i in range(planes)]
                )
            total = part if total is None else total + part
        return total

    sums_in = lax.all_to_all(sums_out, ("brick", "plane"), split_axis=0, concat_axis=0, tiled=True)
    placed = to_owners(jnp.stack([charge_row, hardness_row, field]))
    global_sums = jnp.sum(sums_in, axis=0)
    potential_level = (global_sums[0] + global_sums[1]) / global_sums[2]
    charges = (potential_level - field) / hardness_row
    placed_aux = placed[0]
    placed_charges = (potential_level - placed[2]) / placed[1]
    previous = aux_prev.reshape(tile_count, TILE)
    next_aux = 2.0 * placed_aux - previous + kappa * (placed_charges - placed_aux)
    return (charges.reshape(aux.shape), next_aux.reshape(aux.shape), resid_field.reshape(aux.shape))


def solution(mesh):
    in_specs = (
        P("brick", "plane", None, None),
        P("brick", "plane", None),
        P("brick", "plane", None),
        P("brick", "plane", None),
        P("brick", "plane", None),
        P("brick", "plane", None),
        P("brick", "plane", None),
        P("brick", "plane"),
        P("brick", "plane", None),
        P(),
        P(),
        P(),
    )
    out_specs = (P("brick", "plane", None), P("brick", "plane", None), P("brick", "plane", None))
    return jax.shard_map(
        on_device, mesh=mesh, in_specs=in_specs, out_specs=out_specs, check_vma=False
    )
```
